32 devices in a mesh: ch: 8 (over y, x, core), row: 4 (over z).
Axes of the slice: x: 2, y: 2, z: 4, core: 2. Of those that a mesh axis runs over, the one named last changes fastest.
Arguments:
- eta_pp: bfloat16 [32, 1024, 1024], P('ch', 'row'), as said below
- gamma_pp: bfloat16 [32, 1024, 1024], P('ch', 'row'), as said below
- pp_factor: int32 [32, 1024], P('ch'), may hold values from -1 to 1
- ph_factor: int32 [32, 1024], P(('ch', 'row')), may hold values from -1 to 1
- recouple: float32 [32, 1024], P(('ch', 'row')), may hold values from -1.5 to 1.5
- src_slot: int32 [32, 8], replicated, may hold values from 0 to 3
Outputs:
- dgamma: bfloat16 [32, 1024, 1024], P('ch', 'row')
The draws below stay inside these ranges and needn't reach their ends.
Inputs may be any that keep to these rules, and one draw needn't show every extreme that they name: Every block eta_pp[c] is antisymmetric: eta_pp[c][i, k] = -eta_pp[c][k, i]. Every block gamma_pp[c] is symmetric.
All inputs are finite; a program needn't handle non-finite values.
Results may differ from the reference program's by a relative error of at most 0.0033.
Values may be sent and summed in bfloat16 or wider, within the bound.
No kernel may reach another device: no remote copies, remote signals or barrier semaphores. Data moves between devices by JAX's collectives and lax.ppermute only.
A program may use at most 128 MiB of HBM per device.

```python
import jax
import jax.numpy as jnp
from jax import lax

PP = 1024
CH_DEV = 4
NCH = 32
N_CH = 8


def base_matrix(key):
    return jax.random.normal(key, (NCH, PP, PP), jnp.float32)


def draw_eta_pp(key, part):
    values = base_matrix(jax.random.fold_in(key, 11))
    return ((values - jnp.swapaxes(values, 1, 2)) * (2.0 * PP) ** (-0.5)).astype(jnp.bfloat16)


def draw_gamma_pp(key, part):
    values = base_matrix(jax.random.fold_in(key, 23))
    return ((values + jnp.swapaxes(values, 1, 2)) * 0.5 ** 0.5).astype(jnp.bfloat16)


def touch_ends(array, stream_key, smallest, largest):
    dims = array.shape
    place = [jax.random.randint(jax.random.fold_in(stream_key, axis), (), 0, dims[axis]) for axis in range(len(dims))]
    array = array.at[tuple(place)].set(smallest)
    longest = dims.index(max(dims))
    place[longest] = (place[longest] + 1) % dims[longest]
    return array.at[tuple(place)].set(largest)


def level_of(rng, extent, split, least, high):
    gain = 1.0
    for dim, blocks in split:
        steps = jax.random.uniform(jax.random.fold_in(jax.random.fold_in(rng, 6), dim), (blocks,), jnp.float32, least / len(split), high / len(split))
        gain = gain * jnp.repeat(jnp.exp(steps), extent[dim] // blocks).reshape((-1,) + (1,) * (len(extent) - 1 - dim))
    return gain


def setup_inputs(seed: int = 0) -> dict:
    keys = jax.random.split(jax.random.key(seed), 7)
    eta_pp = draw_eta_pp(jax.random.fold_in(keys[6], 71), 0)
    gamma_pp = draw_gamma_pp(jax.random.fold_in(keys[6], 71), 0)
    pp_factor = touch_ends(jax.random.randint(keys[2], (NCH, PP), -1, 2), jax.random.fold_in(keys[2], 1), -1, 1).astype(jnp.int32)
    ph_factor = touch_ends(jax.random.randint(keys[3], (NCH, PP), -1, 2), jax.random.fold_in(keys[3], 1), -1, 1).astype(jnp.int32)
    recouple = jnp.clip(jax.random.uniform(keys[4], (NCH, PP), jnp.float32, -1.5, 1.5) * level_of(keys[4], (NCH, PP), ((0, 32),), -0.4, 0.0), -1.5, 1.5)
    src_slot = touch_ends(jax.random.randint(keys[5], (NCH, N_CH), 0, CH_DEV), jax.random.fold_in(keys[5], 1), 0, CH_DEV - 1).astype(jnp.int32)
    return dict(eta_pp=eta_pp, gamma_pp=gamma_pp, pp_factor=pp_factor, ph_factor=ph_factor, recouple=recouple, src_slot=src_slot)


def reference(eta_pp, gamma_pp, pp_factor, ph_factor, recouple, src_slot):
    f32 = jnp.float32
    highest = lax.Precision.HIGHEST
    slab = PP // N_CH

    def ladder_one(items):
        eta, gamma, factor = items
        eta_f = eta.astype(f32)
        gamma_f = gamma.astype(f32)
        first = jnp.dot(eta_f * factor[None, :], gamma_f, precision=highest)
        second = jnp.dot(gamma_f * factor[None, :], eta_f, precision=highest)
        return first - second

    ladder = lax.map(ladder_one, (eta_pp, gamma_pp, pp_factor.astype(f32)))

    eta_five = eta_pp.reshape(N_CH, CH_DEV, PP, N_CH, slab)
    gamma_five = gamma_pp.reshape(N_CH, CH_DEV, PP, N_CH, slab)
    sources = jnp.arange(N_CH, dtype=jnp.int32)

    def ph_one(items):
        block, factor, coef = items
        group = (block // CH_DEV).astype(jnp.int32)
        slots = src_slot[block]
        eta_sub = lax.dynamic_index_in_dim(eta_five, group, 3, False)[sources, slots]
        gamma_sub = lax.dynamic_index_in_dim(gamma_five, group, 3, False)[sources, slots]
        eta_ph = eta_sub.transpose(1, 0, 2).reshape(PP, PP).astype(f32)
        gamma_ph = gamma_sub.transpose(1, 0, 2).reshape(PP, PP).astype(f32)
        first = jnp.dot(eta_ph * factor[None, :], gamma_ph, precision=highest)
        second = jnp.dot(gamma_ph * factor[None, :], eta_ph, precision=highest)
        return ((first - second) * coef[None, :]).astype(jnp.bfloat16)

    ph_term = lax.map(ph_one, (jnp.arange(NCH, dtype=jnp.int32), ph_factor.astype(f32), recouple))
    term_five = ph_term.reshape(N_CH, CH_DEV, PP, N_CH, slab)
    selected = (src_slot.reshape(N_CH, CH_DEV, N_CH)[..., None] == jnp.arange(CH_DEV, dtype=jnp.int32)).astype(f32)

    def back_one(source):
        terms = lax.dynamic_index_in_dim(term_five, source, 3, False).astype(f32)
        picks = lax.dynamic_index_in_dim(selected, source, 2, False)
        summed = jnp.einsum('gqs,gqiw->sigw', picks, terms, precision=highest)
        return summed.reshape(CH_DEV, PP, PP)

    back = lax.map(back_one, sources).reshape(NCH, PP, PP)
    return (ladder + back).astype(jnp.bfloat16)
```

```python
import jax
import jax.numpy as jnp
from jax import lax
from jax.sharding import PartitionSpec as P


def per_device(eta_pp, gamma_pp, pp_factor, ph_factor, recouple, src_slot):
    f32 = jnp.float32
    bf16 = jnp.bfloat16
    n_chan = lax.axis_size("ch")
    n_rows = lax.axis_size("row")
    ch_dev, rows, width = eta_pp.shape
    slab = width // n_chan
    n_total = ch_dev * n_chan
    assert ch_dev == n_rows and rows % slab == 0 and n_chan * slab == width
    mine = lax.axis_index("ch")
    level = lax.axis_index("row")

    stacked = jnp.stack([eta_pp, gamma_pp])
    whole = lax.all_to_all(stacked, "row", split_axis=1, concat_axis=2, tiled=True)
    eta_c = whole[0, 0]
    gamma_c = whole[1, 0]

    dest = jnp.arange(n_chan, dtype=jnp.int32)
    q_dest = level * n_chan + dest
    slot_dest = src_slot[q_dest, mine]
    part_dest = q_dest // ch_dev - level * (rows // slab)
    five = stacked.reshape(2, ch_dev, rows // slab, slab, width)
    outgoing = five[:, slot_dest, part_dest]
    arrived = lax.all_to_all(outgoing, "ch", split_axis=1, concat_axis=1, tiled=True)
    a_eta = arrived[0].reshape(width, width)
    b_gamma = arrived[1].reshape(width, width)

    perm = [(q, (q % n_chan) * n_rows + q // n_chan) for q in range(n_total)]
    coefs = lax.ppermute(
        jnp.concatenate([ph_factor.astype(f32), recouple], axis=0), ("ch", "row"), perm
    )
    weight = coefs[0].astype(bf16)[None, :]
    coef = coefs[1]

    ph_t = jnp.dot(a_eta * weight, b_gamma, preferred_element_type=f32)
    ph_t = ph_t - jnp.dot(b_gamma * weight, a_eta, preferred_element_type=f32)
    term_t = (ph_t * coef[:, None]).astype(bf16)
    returning = term_t.reshape(n_chan, slab, n_rows, rows).transpose(0, 2, 1, 3)
    landed = lax.all_to_all(
        returning.reshape(n_chan * n_rows, slab, rows),
        ("ch", "row"),
        split_axis=0,
        concat_axis=0,
        tiled=True,
    )
    landed = landed.reshape(n_chan, n_rows, slab, rows).transpose(1, 0, 2, 3)
    landed = landed.reshape(n_chan, ch_dev, slab, rows)
    chosen = src_slot[:, mine].reshape(n_chan, ch_dev)
    onehot = (chosen[:, :, None] == jnp.arange(ch_dev, dtype=jnp.int32)[None, None, :]).astype(bf16)
    back = jnp.einsum("gts,gtwi->sigw", onehot, landed, preferred_element_type=f32)
    back = back.reshape(ch_dev, rows, width)

    factor = lax.dynamic_index_in_dim(pp_factor, level, 0, False).astype(bf16)
    product = jnp.dot(eta_c * factor[None, :], gamma_c, preferred_element_type=f32)
    ladder_c = product + product.T
    ladder = lax.all_to_all(
        ladder_c.reshape(n_rows, rows, width), "row", split_axis=0, concat_axis=0, tiled=True
    )
    return (ladder + back).astype(bf16)


def solution(mesh):
    placed = (
        P("ch", "row", None),
        P("ch", "row", None),
        P("ch", None),
        P(("ch", "row"), None),
        P(("ch", "row"), None),
        P(),
    )
    return jax.shard_map(
        per_device, mesh=mesh, in_specs=placed, out_specs=P("ch", "row", None), check_vma=False
    )
```

```python
import jax
import jax.numpy as jnp
from jax import lax
from jax.sharding import PartitionSpec as P


def skip_block(x, b, size):
    return jnp.concatenate([x[..., (b + 1) * size :], x[..., : b * size]], axis=-1)


def per_device(eta_pp, gamma_pp, pp_factor, ph_factor, recouple, src_slot):
    f32 = jnp.float32
    bf16 = jnp.bfloat16
    n_chan = lax.axis_size("ch")
    n_rows = lax.axis_size("row")
    ch_dev, rows, width = eta_pp.shape
    slab = width // n_chan
    n_total = ch_dev * n_chan
    assert ch_dev == n_rows and rows % slab == 0 and n_chan * slab == width
    mine = lax.axis_index("ch")
    level = lax.axis_index("row")

    stacked = jnp.stack([eta_pp, gamma_pp])
    sending = jnp.stack(
        [skip_block(stacked[:, s], s, rows) for s in range(n_rows)], axis=1
    )
    whole = lax.all_to_all(sending, "row", split_axis=1, concat_axis=1, tiled=True)
    own = lax.dynamic_index_in_dim(stacked, level, 1, False)
    own_t = own.reshape(2, rows, n_rows, rows).transpose(0, 2, 3, 1)
    own_t = own_t * jnp.array([-1, 1], bf16)[:, None, None, None]
    whole = jnp.concatenate([whole, own_t], axis=-1)
    whole = jnp.roll(whole, (level + 1) * rows, axis=-1).reshape(2, width, width)
    eta_c = whole[0]
    gamma_c = whole[1]

    dest = jnp.arange(n_chan, dtype=jnp.int32)
    q_dest = level * n_chan + dest
    slot_dest = src_slot[q_dest, mine]
    part_dest = q_dest // ch_dev - level * (rows // slab)
    five = stacked.reshape(2, ch_dev, rows // slab, slab, width)
    outgoing = five[:, slot_dest, part_dest]
    pieces = [lax.dynamic_index_in_dim(outgoing, mine, 1, False)]
    for shift in range(1, n_chan):
        piece = lax.dynamic_index_in_dim(outgoing, (mine + shift) % n_chan, 1, False)
        pairs = [(a, (a + shift) % n_chan) for a in range(n_chan)]
        pieces.append(lax.ppermute(piece, "ch", pairs))
    arrived = jnp.stack(pieces, axis=1)[:, (mine - dest) % n_chan]
    a_eta = arrived[0].reshape(width, width)
    b_gamma = arrived[1].reshape(width, width)

    perm = [(q, (q % n_chan) * n_rows + q // n_chan) for q in range(n_total)]
    coefs = lax.ppermute(
        jnp.concatenate([ph_factor.astype(f32), recouple], axis=0), ("ch", "row"), perm
    )
    weight = coefs[0].astype(bf16)[None, :]
    coef = coefs[1]

    ph_t = jnp.dot(a_eta * weight, b_gamma, preferred_element_type=f32)
    ph_t = ph_t - jnp.dot(b_gamma * weight, a_eta, preferred_element_type=f32)
    term_t = (ph_t * coef[:, None]).astype(bf16)
    returning = term_t.reshape(n_chan, slab, n_rows, rows).transpose(0, 2, 1, 3)
    landed = lax.all_to_all(
        returning.reshape(n_chan * n_rows, slab, rows),
        ("ch", "row"),
        split_axis=0,
        concat_axis=0,
        tiled=True,
    )
    landed = landed.reshape(n_chan, n_rows, slab, rows).transpose(1, 0, 2, 3)
    landed = landed.reshape(n_chan, ch_dev, slab, rows)
    chosen = src_slot[:, mine].reshape(n_chan, ch_dev)
    onehot = (chosen[:, :, None] == jnp.arange(ch_dev, dtype=jnp.int32)[None, None, :]).astype(bf16)
    back = jnp.einsum("gts,gtwi->sigw", onehot, landed, preferred_element_type=f32)
    back = back.reshape(ch_dev, rows, width)

    factor = lax.dynamic_index_in_dim(pp_factor, level, 0, False).astype(bf16)
    product = jnp.dot(eta_c * factor[None, :], gamma_c, preferred_element_type=f32)
    ladder_c = (product + product.T).reshape(n_rows, rows, width)
    sending = jnp.stack([skip_block(ladder_c[a], a, rows) for a in range(n_rows)])
    ladder = lax.all_to_all(sending, "row", split_axis=0, concat_axis=0, tiled=True)
    weighted = eta_pp * pp_factor.astype(bf16)[:, None, :]
    diag = jnp.einsum("sik,sjk->sij", weighted, gamma_pp, preferred_element_type=f32)
    diag = diag + jnp.swapaxes(diag, 1, 2)
    ladder = jnp.concatenate([ladder, diag], axis=-1)
    ladder = jnp.roll(ladder, (level + 1) * rows, axis=-1)
    return (ladder + back).astype(bf16)


def solution(mesh):
    placed = (
        P("ch", "row", None),
        P("ch", "row", None),
        P("ch", None),
        P(("ch", "row"), None),
        P(("ch", "row"), None),
        P(),
    )
    return jax.shard_map(
        per_device, mesh=mesh, in_specs=placed, out_specs=P("ch", "row", None), check_vma=False
    )
```

```python
import jax
import jax.numpy as jnp
from jax import lax
from jax.sharding import PartitionSpec as P


def skip_block(x, b, size):
    return jnp.concatenate([x[..., (b + 1) * size :], x[..., : b * size]], axis=-1)


def per_device(eta_pp, gamma_pp, pp_factor, ph_factor, recouple, src_slot):
    f32 = jnp.float32
    bf16 = jnp.bfloat16
    n_chan = lax.axis_size("ch")
    n_rows = lax.axis_size("row")
    ch_dev, rows, width = eta_pp.shape
    slab = width // n_chan
    n_total = ch_dev * n_chan
    assert ch_dev == n_rows and rows % slab == 0 and n_chan * slab == width
    mine = lax.axis_index("ch")
    level = lax.axis_index("row")

    stacked = jnp.stack([eta_pp, gamma_pp])
    sending = jnp.stack(
        [skip_block(stacked[:, s], s, rows) for s in range(n_rows)], axis=1
    )
    whole = lax.all_to_all(sending, "row", split_axis=1, concat_axis=1, tiled=True)
    dest = jnp.arange(n_chan, dtype=jnp.int32)
    q_dest = level * n_chan + dest
    slot_dest = src_slot[q_dest, mine]
    part_dest = q_dest // ch_dev - level * (rows // slab)
    five = stacked.reshape(2, ch_dev, rows // slab, slab, width)
    outgoing = five[:, slot_dest, part_dest]
    pieces = [lax.dynamic_index_in_dim(outgoing, mine, 1, False)]
    for shift in range(1, n_chan):
        piece = lax.dynamic_index_in_dim(outgoing, (mine + shift) % n_chan, 1, False)
        pairs = [(a, (a + shift) % n_chan) for a in range(n_chan)]
        pieces.append(lax.ppermute(piece, "ch", pairs))
    whole, pieces = lax.optimization_barrier((whole, pieces))
    arrived = jnp.stack(pieces, axis=1)[:, (mine - dest) % n_chan]
    a_eta = arrived[0].reshape(width, width)
    b_gamma = arrived[1].reshape(width, width)

    own = lax.dynamic_index_in_dim(stacked, level, 1, False)
    own_t = own.reshape(2, rows, n_rows, rows).transpose(0, 2, 3, 1)
    own_t = own_t * jnp.array([-1, 1], bf16)[:, None, None, None]
    whole = jnp.concatenate([whole, own_t], axis=-1)
    whole = jnp.roll(whole, (level + 1) * rows, axis=-1).reshape(2, width, width)
    eta_c = whole[0]
    gamma_c = whole[1]

    factor = lax.dynamic_index_in_dim(pp_factor, level, 0, False).astype(bf16)
    product = jnp.dot(eta_c * factor[None, :], gamma_c, preferred_element_type=f32)
    ladder_c = (product + product.T).reshape(n_rows, rows, width)
    sending = jnp.stack([skip_block(ladder_c[a], a, rows) for a in range(n_rows)])
    ladder = lax.all_to_all(sending, "row", split_axis=0, concat_axis=0, tiled=True)
    perm = [(q, (q % n_chan) * n_rows + q // n_chan) for q in range(n_total)]
    coefs = lax.ppermute(
        jnp.concatenate([ph_factor.astype(f32), recouple], axis=0), ("ch", "row"), perm
    )
    weight = coefs[0].astype(bf16)[None, :]
    coef = coefs[1]

    ph_t = jnp.dot(a_eta * weight, b_gamma, preferred_element_type=f32)
    ph_t = ph_t - jnp.dot(b_gamma * weight, a_eta, preferred_element_type=f32)
    term_t = (ph_t * coef[:, None]).astype(bf16)
    ladder, term_t = lax.optimization_barrier((ladder, term_t))
    returning = term_t.reshape(n_chan, slab, n_rows, rows).transpose(0, 2, 1, 3)
    landed = lax.all_to_all(
        returning.reshape(n_chan * n_rows, slab, rows),
        ("ch", "row"),
        split_axis=0,
        concat_axis=0,
        tiled=True,
    )
    landed = landed.reshape(n_chan, n_rows, slab, rows).transpose(1, 0, 2, 3)
    landed = landed.reshape(n_chan, ch_dev, slab, rows)
    chosen = src_slot[:, mine].reshape(n_chan, ch_dev)
    onehot = (chosen[:, :, None] == jnp.arange(ch_dev, dtype=jnp.int32)[None, None, :]).astype(bf16)
    back = jnp.einsum("gts,gtwi->sigw", onehot, landed, preferred_element_type=f32)
    back = back.reshape(ch_dev, rows, width)

    weighted = eta_pp * pp_factor.astype(bf16)[:, None, :]
    diag = jnp.einsum("sik,sjk->sij", weighted, gamma_pp, preferred_element_type=f32)
    diag = diag + jnp.swapaxes(diag, 1, 2)
    ladder = jnp.concatenate([ladder, diag], axis=-1)
    ladder = jnp.roll(ladder, (level + 1) * rows, axis=-1)
    return (ladder + back).astype(bf16)


def solution(mesh):
    placed = (
        P("ch", "row", None),
        P("ch", "row", None),
        P("ch", None),
        P(("ch", "row"), None),
        P(("ch", "row"), None),
        P(),
    )
    return jax.shard_map(
        per_device, mesh=mesh, in_specs=placed, out_specs=P("ch", "row", None), check_vma=False
    )
```

```python
import jax
import jax.numpy as jnp
from jax import lax
from jax.sharding import PartitionSpec as P


def skip_block(x, b, size):
    return jnp.concatenate([x[..., (b + 1) * size :], x[..., : b * size]], axis=-1)


def per_device(eta_pp, gamma_pp, pp_factor, ph_factor, recouple, src_slot):
    f32 = jnp.float32
    bf16 = jnp.bfloat16
    n_chan = lax.axis_size("ch")
    n_rows = lax.axis_size("row")
    ch_dev, rows, width = eta_pp.shape
    slab = width // n_chan
    n_total = ch_dev * n_chan
    assert ch_dev == n_rows and rows % slab == 0 and n_chan * slab == width
    mine = lax.axis_index("ch")
    level = lax.axis_index("row")

    stacked = jnp.stack([eta_pp, gamma_pp])
    sending = jnp.stack(
        [skip_block(stacked[:, s], s, rows) for s in range(n_rows)], axis=1
    )
    whole = lax.all_to_all(sending, "row", split_axis=1, concat_axis=1, tiled=True)
    dest = jnp.arange(n_chan, dtype=jnp.int32)
    q_dest = level * n_chan + dest
    slot_dest = src_slot[q_dest, mine]
    part_dest = q_dest // ch_dev - level * (rows // slab)
    five = stacked.reshape(2, ch_dev, rows // slab, slab, width)
    outgoing = five[:, slot_dest, part_dest]
    pieces = [lax.dynamic_index_in_dim(outgoing, mine, 1, True)]
    for shift in range(1, n_chan):
        piece = lax.dynamic_index_in_dim(outgoing, (mine + shift) % n_chan, 1, True)
        pairs = [(a, (a + shift) % n_chan) for a in range(n_chan)]
        pieces.append(lax.ppermute(piece, "ch", pairs))
    whole, pieces = lax.optimization_barrier((whole, pieces))
    arrived = jnp.concatenate(pieces, axis=1)[:, (mine - dest) % n_chan]
    a_eta = arrived[0].reshape(width, width)
    b_gamma = arrived[1].reshape(width, width)

    perm = [(q, (q % n_chan) * n_rows + q // n_chan) for q in range(n_total)]
    coefs = lax.ppermute(
        jnp.concatenate([ph_factor.astype(f32), recouple], axis=0), ("ch", "row"), perm
    )
    weight = coefs[0].astype(bf16)[None, :]
    coef = coefs[1]

    ph_t = jnp.dot(a_eta * weight, b_gamma, preferred_element_type=f32)
    ph_t = ph_t - jnp.dot(b_gamma * weight, a_eta, preferred_element_type=f32)
    term_t = (ph_t * coef[:, None]).astype(bf16)
    whole, term_t = lax.optimization_barrier((whole, term_t))
    own = lax.dynamic_index_in_dim(stacked, level, 1, False)
    own_t = own.reshape(2, rows, n_rows, rows).transpose(0, 2, 3, 1)
    own_t = own_t * jnp.array([-1, 1], bf16)[:, None, None, None]
    whole = jnp.concatenate([whole, own_t], axis=-1)
    whole = jnp.roll(whole, (level + 1) * rows, axis=-1).reshape(2, width, width)
    eta_c = whole[0]
    gamma_c = whole[1]

    factor = lax.dynamic_index_in_dim(pp_factor, level, 0, False).astype(bf16)
    product = jnp.dot(eta_c * factor[None, :], gamma_c, preferred_element_type=f32)
    ladder_c = (product + product.T).reshape(n_rows, rows, width)
    sending = jnp.stack([skip_block(ladder_c[a], a, rows) for a in range(n_rows)])
    returning = term_t.reshape(n_chan, slab, n_rows, rows).transpose(0, 2, 1, 3)
    landed = lax.all_to_all(
        returning.reshape(n_chan * n_rows, slab, rows),
        ("ch", "row"),
        split_axis=0,
        concat_axis=0,
        tiled=True,
    )
    landed = landed.reshape(n_chan, n_rows, slab, rows).transpose(1, 0, 2, 3)
    landed = landed.reshape(n_chan, ch_dev, slab, rows)
    sending, landed = lax.optimization_barrier((sending, landed))
    ladder = lax.all_to_all(sending, "row", split_axis=0, concat_axis=0, tiled=True)
    chosen = src_slot[:, mine].reshape(n_chan, ch_dev)
    onehot = (chosen[:, :, None] == jnp.arange(ch_dev, dtype=jnp.int32)[None, None, :]).astype(bf16)
    back = jnp.einsum("gts,gtwi->sigw", onehot, landed, preferred_element_type=f32)
    back = back.reshape(ch_dev, rows, width)

    weighted = eta_pp * pp_factor.astype(bf16)[:, None, :]
    diag = jnp.einsum("sik,sjk->sij", weighted, gamma_pp, preferred_element_type=f32)
    diag = diag + jnp.swapaxes(diag, 1, 2)
    ladder = jnp.concatenate([ladder, diag], axis=-1)
    ladder = jnp.roll(ladder, (level + 1) * rows, axis=-1)
    return (ladder + back).astype(bf16)


def solution(mesh):
    placed = (
        P("ch", "row", None),
        P("ch", "row", None),
        P("ch", None),
        P(("ch", "row"), None),
        P(("ch", "row"), None),
        P(),
    )
    return jax.shard_map(
        per_device, mesh=mesh, in_specs=placed, out_specs=P("ch", "row", None), check_vma=False
    )
```

```python
import jax
import jax.numpy as jnp
from jax import lax
from jax.sharding import PartitionSpec as P


def skip_block(x, b, size):
    return jnp.concatenate([x[..., (b + 1) * size :], x[..., : b * size]], axis=-1)


def per_device(eta_pp, gamma_pp, pp_factor, ph_factor, recouple, src_slot):
    f32 = jnp.float32
    bf16 = jnp.bfloat16
    n_chan = lax.axis_size("ch")
    n_rows = lax.axis_size("row")
    ch_dev, rows, width = eta_pp.shape
    slab = width // n_chan
    n_total = ch_dev * n_chan
    assert ch_dev == n_rows and rows % slab == 0 and n_chan * slab == width
    mine = lax.axis_index("ch")
    level = lax.axis_index("row")

    stacked = jnp.stack([eta_pp, gamma_pp])
    sending = jnp.stack(
        [skip_block(stacked[:, s], s, rows) for s in range(n_rows)], axis=1
    )
    whole = lax.all_to_all(sending, "row", split_axis=1, concat_axis=1, tiled=True)
    dest = jnp.arange(n_chan, dtype=jnp.int32)
    q_dest = level * n_chan + dest
    slot_dest = src_slot[q_dest, mine]
    part_dest = q_dest // ch_dev - level * (rows // slab)
    five = stacked.reshape(2, ch_dev, rows // slab, slab, width)
    outgoing = five[:, slot_dest, part_dest]
    pieces = [lax.dynamic_index_in_dim(outgoing, mine, 1, False)]
    for shift in range(1, n_chan):
        piece = lax.dynamic_index_in_dim(outgoing, (mine + shift) % n_chan, 1, False)
        pairs = [(a, (a + shift) % n_chan) for a in range(n_chan)]
        pieces.append(lax.ppermute(piece, "ch", pairs))
    whole, pieces = lax.optimization_barrier((whole, pieces))
    arrived = jnp.stack(pieces, axis=1)[:, (mine - dest) % n_chan]
    a_eta = arrived[0].reshape(width, width)
    b_gamma = arrived[1].reshape(width, width)

    perm = [(q, (q % n_chan) * n_rows + q // n_chan) for q in range(n_total)]
    coefs = lax.ppermute(
        jnp.concatenate([ph_factor.astype(f32), recouple], axis=0), ("ch", "row"), perm
    )
    weight = coefs[0].astype(bf16)[None, :]
    coef = coefs[1]

    ph_t = jnp.dot(a_eta * weight, b_gamma, preferred_element_type=f32)
    ph_t = ph_t - jnp.dot(b_gamma * weight, a_eta, preferred_element_type=f32)
    term_t = (ph_t * coef[:, None]).astype(bf16)
    whole, term_t = lax.optimization_barrier((whole, term_t))
    own = lax.dynamic_index_in_dim(stacked, level, 1, False)
    own_t = own.reshape(2, rows, n_rows, rows).transpose(0, 2, 3, 1)
    own_t = own_t * jnp.array([-1, 1], bf16)[:, None, None, None]
    whole = jnp.concatenate([whole, own_t], axis=-1).reshape(2, width, width)
    factor = lax.dynamic_index_in_dim(pp_factor, level, 0, False).astype(bf16)
    factor = jnp.roll(factor, -(level + 1) * rows)
    left = jnp.concatenate([whole[0] * factor, whole[1] * factor], axis=-1)
    right = jnp.concatenate([whole[1], whole[0]], axis=-1)
    ladder_c = lax.dot_general(
        left, right, (((1,), (1,)), ((), ())), preferred_element_type=f32
    ).reshape(n_rows, rows, width)
    sending = jnp.stack([skip_block(ladder_c[a], a, rows) for a in range(n_rows)])
    returning = term_t.reshape(n_chan, slab, n_rows, rows).transpose(0, 2, 1, 3)
    landed = lax.all_to_all(
        returning.reshape(n_chan * n_rows, slab, rows),
        ("ch", "row"),
        split_axis=0,
        concat_axis=0,
        tiled=True,
    )
    landed = landed.reshape(n_chan, n_rows, slab, rows).transpose(1, 0, 2, 3)
    landed = landed.reshape(n_chan, ch_dev, slab, rows)
    sending, landed = lax.optimization_barrier((sending, landed))
    ladder = lax.all_to_all(sending, "row", split_axis=0, concat_axis=0, tiled=True)
    chosen = src_slot[:, mine].reshape(n_chan, ch_dev)
    onehot = (chosen[:, :, None] == jnp.arange(ch_dev, dtype=jnp.int32)[None, None, :]).astype(bf16)
    back = jnp.einsum("gts,gtwi->sigw", onehot, landed, preferred_element_type=f32)
    back = back.reshape(ch_dev, rows, width)

    local_d = pp_factor.astype(bf16)[:, None, :]
    left = jnp.concatenate([eta_pp * local_d, gamma_pp * local_d], axis=-1)
    right = jnp.concatenate([gamma_pp, eta_pp], axis=-1)
    diag = jnp.einsum("sik,sjk->sij", left, right, preferred_element_type=f32)
    ladder = jnp.concatenate([ladder, diag], axis=-1)
    ladder = jnp.roll(ladder, (level + 1) * rows, axis=-1)
    return (ladder + back).astype(bf16)


def solution(mesh):
    placed = (
        P("ch", "row", None),
        P("ch", "row", None),
        P("ch", None),
        P(("ch", "row"), None),
        P(("ch", "row"), None),
        P(),
    )
    return jax.shard_map(
        per_device, mesh=mesh, in_specs=placed, out_specs=P("ch", "row", None), check_vma=False
    )
```

```python
import jax
import jax.numpy as jnp
from jax import lax
from jax.sharding import PartitionSpec as P


def skip_block(x, b, size):
    return jnp.concatenate([x[..., (b + 1) * size :], x[..., : b * size]], axis=-1)


def per_device(eta_pp, gamma_pp, pp_factor, ph_factor, recouple, src_slot):
    f32 = jnp.float32
    bf16 = jnp.bfloat16
    n_chan = lax.axis_size("ch")
    n_rows = lax.axis_size("row")
    ch_dev, rows, width = eta_pp.shape
    slab = width // n_chan
    n_total = ch_dev * n_chan
    assert ch_dev == n_rows and rows % slab == 0 and n_chan * slab == width
    mine = lax.axis_index("ch")
    level = lax.axis_index("row")

    stacked = jnp.stack([eta_pp, gamma_pp])
    sending = jnp.stack(
        [skip_block(stacked[:, s], s, rows) for s in range(n_rows)], axis=1
    )
    ladder_in = [lax.dynamic_index_in_dim(sending, level, 1, False)]
    for shift in range(1, n_rows):
        piece = lax.dynamic_index_in_dim(sending, (level + shift) % n_rows, 1, False)
        pairs = [(a, (a + shift) % n_rows) for a in range(n_rows)]
        ladder_in.append(lax.ppermute(piece, "row", pairs))
    dest = jnp.arange(n_chan, dtype=jnp.int32)
    q_dest = level * n_chan + dest
    slot_dest = src_slot[q_dest, mine]
    part_dest = q_dest // ch_dev - level * (rows // slab)
    five = stacked.reshape(2, ch_dev, rows // slab, slab, width)
    outgoing = five[:, slot_dest, part_dest]
    arrived = lax.all_to_all(outgoing, "ch", split_axis=1, concat_axis=1, tiled=True)
    a_eta = arrived[0].reshape(width, width)
    b_gamma = arrived[1].reshape(width, width)

    perm = [(q, (q % n_chan) * n_rows + q // n_chan) for q in range(n_total)]
    coefs = lax.ppermute(
        jnp.concatenate([ph_factor.astype(f32), recouple], axis=0), ("ch", "row"), perm
    )
    weight = coefs[0].astype(bf16)[None, :]
    coef = coefs[1]

    ph_t = jnp.dot(a_eta * weight, b_gamma, preferred_element_type=f32)
    ph_t = ph_t - jnp.dot(b_gamma * weight, a_eta, preferred_element_type=f32)
    term_t = (ph_t * coef[:, None]).astype(bf16)
    ladder_in, term_t = lax.optimization_barrier((ladder_in, term_t))
    sources = (level - jnp.arange(n_rows, dtype=jnp.int32)) % n_rows
    whole = jnp.stack(ladder_in, axis=1)[:, sources]
    own = lax.dynamic_index_in_dim(stacked, level, 1, False)
    own_t = own.reshape(2, rows, n_rows, rows).transpose(0, 2, 3, 1)
    own_t = own_t * jnp.array([-1, 1], bf16)[:, None, None, None]
    whole = jnp.concatenate([whole, own_t], axis=-1).reshape(2, width, width)
    factor = lax.dynamic_index_in_dim(pp_factor, level, 0, False).astype(bf16)
    factor = jnp.roll(factor, -(level + 1) * rows)
    left = jnp.concatenate([whole[0] * factor, whole[1] * factor], axis=-1)
    right = jnp.concatenate([whole[1], whole[0]], axis=-1)
    ladder_c = lax.dot_general(
        left, right, (((1,), (1,)), ((), ())), preferred_element_type=f32
    ).reshape(n_rows, rows, width)
    sending = jnp.stack([skip_block(ladder_c[a], a, rows) for a in range(n_rows)])
    returning = term_t.reshape(n_chan, slab, n_rows, rows).transpose(0, 2, 1, 3)
    landed = lax.all_to_all(
        returning.reshape(n_chan * n_rows, slab, rows),
        ("ch", "row"),
        split_axis=0,
        concat_axis=0,
        tiled=True,
    )
    landed = landed.reshape(n_chan, n_rows, slab, rows).transpose(1, 0, 2, 3)
    landed = landed.reshape(n_chan, ch_dev, slab, rows)
    sending, landed = lax.optimization_barrier((sending, landed))
    ladder = lax.all_to_all(sending, "row", split_axis=0, concat_axis=0, tiled=True)
    chosen = src_slot[:, mine].reshape(n_chan, ch_dev)
    onehot = (chosen[:, :, None] == jnp.arange(ch_dev, dtype=jnp.int32)[None, None, :]).astype(bf16)
    back = jnp.einsum("gts,gtwi->sigw", onehot, landed, preferred_element_type=f32)
    back = back.reshape(ch_dev, rows, width)

    local_d = pp_factor.astype(bf16)[:, None, :]
    left = jnp.concatenate([eta_pp * local_d, gamma_pp * local_d], axis=-1)
    right = jnp.concatenate([gamma_pp, eta_pp], axis=-1)
    diag = jnp.einsum("sik,sjk->sij", left, right, preferred_element_type=f32)
    ladder = jnp.concatenate([ladder, diag], axis=-1)
    ladder = jnp.roll(ladder, (level + 1) * rows, axis=-1)
    return (ladder + back).astype(bf16)


def solution(mesh):
    placed = (
        P("ch", "row", None),
        P("ch", "row", None),
        P("ch", None),
        P(("ch", "row"), None),
        P(("ch", "row"), None),
        P(),
    )
    return jax.shard_map(
        per_device, mesh=mesh, in_specs=placed, out_specs=P("ch", "row", None), check_vma=False
    )
```

```python
import jax
import jax.numpy as jnp
from jax import lax
from jax.sharding import PartitionSpec as P


def skip_block(x, b, size):
    return jnp.concatenate([x[..., (b + 1) * size :], x[..., : b * size]], axis=-1)


def per_device(eta_pp, gamma_pp, pp_factor, ph_factor, recouple, src_slot):
    f32 = jnp.float32
    bf16 = jnp.bfloat16
    n_chan = lax.axis_size("ch")
    n_rows = lax.axis_size("row")
    ch_dev, rows, width = eta_pp.shape
    slab = width // n_chan
    n_total = ch_dev * n_chan
    assert ch_dev == n_rows and rows % slab == 0 and n_chan * slab == width
    mine = lax.axis_index("ch")
    level = lax.axis_index("row")

    stacked = jnp.stack([eta_pp, gamma_pp])
    sending = jnp.stack(
        [skip_block(stacked[:, s], s, rows) for s in range(n_rows)], axis=1
    )
    ladder_in = [lax.dynamic_index_in_dim(sending, level, 1, False)]
    for shift in range(1, n_rows):
        piece = lax.dynamic_index_in_dim(sending, (level + shift) % n_rows, 1, False)
        pairs = [(a, (a + shift) % n_rows) for a in range(n_rows)]
        ladder_in.append(lax.ppermute(piece, "row", pairs))
    dest = jnp.arange(n_chan, dtype=jnp.int32)
    q_dest = level * n_chan + dest
    slot_dest = src_slot[q_dest, mine]
    part_dest = q_dest // ch_dev - level * (rows // slab)
    five = stacked.reshape(2, ch_dev, rows // slab, slab, width)
    outgoing = five[:, slot_dest, part_dest]
    arrived = lax.all_to_all(outgoing, "ch", split_axis=1, concat_axis=1, tiled=True)
    a_eta = arrived[0].reshape(width, width)
    b_gamma = arrived[1].reshape(width, width)

    perm = [(q, (q % n_chan) * n_rows + q // n_chan) for q in range(n_total)]
    coefs = lax.ppermute(
        jnp.concatenate([ph_factor.astype(f32), recouple], axis=0), ("ch", "row"), perm
    )
    weight = coefs[0].astype(bf16)[None, :]
    coef = coefs[1]

    ph_t = jnp.dot(a_eta * weight, b_gamma, preferred_element_type=f32)
    ph_t = ph_t - jnp.dot(b_gamma * weight, a_eta, preferred_element_type=f32)
    term_t = (ph_t * coef[:, None]).astype(bf16)
    ladder_in, _ = lax.optimization_barrier((ladder_in, term_t))
    sources = (level - jnp.arange(n_rows, dtype=jnp.int32)) % n_rows
    whole = jnp.stack(ladder_in, axis=1)[:, sources]
    own = lax.dynamic_index_in_dim(stacked, level, 1, False)
    own_t = own.reshape(2, rows, n_rows, rows).transpose(0, 2, 3, 1)
    own_t = own_t * jnp.array([-1, 1], bf16)[:, None, None, None]
    whole = jnp.concatenate([whole, own_t], axis=-1).reshape(2, width, width)
    factor = lax.dynamic_index_in_dim(pp_factor, level, 0, False).astype(bf16)
    factor = jnp.roll(factor, -(level + 1) * rows)
    left = jnp.concatenate([whole[0] * factor, whole[1] * factor], axis=-1)
    right = jnp.concatenate([whole[1], whole[0]], axis=-1)
    ladder_c = lax.dot_general(
        left, right, (((1,), (1,)), ((), ())), preferred_element_type=f32
    ).reshape(n_rows, rows, width)
    sending = jnp.stack([skip_block(ladder_c[a], a, rows) for a in range(n_rows)])
    returning = term_t.reshape(n_chan, slab, n_rows, rows).transpose(0, 2, 1, 3)
    landed = lax.all_to_all(
        returning.reshape(n_chan * n_rows, slab, rows),
        ("ch", "row"),
        split_axis=0,
        concat_axis=0,
        tiled=True,
    )
    landed = landed.reshape(n_chan, n_rows, slab, rows).transpose(1, 0, 2, 3)
    landed = landed.reshape(n_chan, ch_dev, slab, rows)
    returned = [lax.dynamic_index_in_dim(sending, level, 0, False)]
    for shift in range(1, n_rows):
        piece = lax.dynamic_index_in_dim(sending, (level + shift) % n_rows, 0, False)
        pairs = [(a, (a + shift) % n_rows) for a in range(n_rows)]
        returned.append(lax.ppermute(piece, "row", pairs))
    ladder = jnp.stack(returned)[sources]
    chosen = src_slot[:, mine].reshape(n_chan, ch_dev)
    onehot = (chosen[:, :, None] == jnp.arange(ch_dev, dtype=jnp.int32)[None, None, :]).astype(bf16)
    back = jnp.einsum("gts,gtwi->sigw", onehot, landed, preferred_element_type=f32)
    back = back.reshape(ch_dev, rows, width)

    local_d = pp_factor.astype(bf16)[:, None, :]
    left = jnp.concatenate([eta_pp * local_d, gamma_pp * local_d], axis=-1)
    right = jnp.concatenate([gamma_pp, eta_pp], axis=-1)
    diag = jnp.einsum("sik,sjk->sij", left, right, preferred_element_type=f32)
    ladder = jnp.concatenate([ladder, diag], axis=-1)
    ladder = jnp.roll(ladder, (level + 1) * rows, axis=-1)
    return (ladder + back).astype(bf16)


def solution(mesh):
    placed = (
        P("ch", "row", None),
        P("ch", "row", None),
        P("ch", None),
        P(("ch", "row"), None),
        P(("ch", "row"), None),
        P(),
    )
    return jax.shard_map(
        per_device, mesh=mesh, in_specs=placed, out_specs=P("ch", "row", None), check_vma=False
    )
```

```python
import jax
import jax.numpy as jnp
from jax import lax
from jax.sharding import PartitionSpec as P


def skip_block(x, b, size):
    return jnp.concatenate([x[..., (b + 1) * size :], x[..., : b * size]], axis=-1)


def per_device(eta_pp, gamma_pp, pp_factor, ph_factor, recouple, src_slot):
    f32 = jnp.float32
    bf16 = jnp.bfloat16
    n_chan = lax.axis_size("ch")
    n_rows = lax.axis_size("row")
    ch_dev, rows, width = eta_pp.shape
    slab = width // n_chan
    n_total = ch_dev * n_chan
    assert ch_dev == n_rows and rows % slab == 0 and n_chan * slab == width
    mine = lax.axis_index("ch")
    level = lax.axis_index("row")

    assert n_rows == 4
    stacked = jnp.stack([eta_pp, gamma_pp])
    ladder_in = []
    for shift in range(1, n_rows):
        block = lax.dynamic_index_in_dim(stacked, (level + shift) % n_rows, 1, False)
        d = n_rows - shift
        hop = (d % (n_rows - 1) + 1 - d) % n_rows
        own_blk = lax.dynamic_slice_in_dim(block, level * rows, rows, axis=-1)
        next_blk = lax.dynamic_slice_in_dim(
            block, ((level + hop) % n_rows) * rows, rows, axis=-1
        )
        pairs = [(a, (a + shift) % n_rows) for a in range(n_rows)]
        ladder_in.append(
            lax.ppermute(jnp.concatenate([own_blk, next_blk], axis=-1), "row", pairs)
        )
    dest = jnp.arange(n_chan, dtype=jnp.int32)
    q_dest = level * n_chan + dest
    slot_dest = src_slot[q_dest, mine]
    part_dest = q_dest // ch_dev - level * (rows // slab)
    five = stacked.reshape(2, ch_dev, rows // slab, slab, width)
    outgoing = five[:, slot_dest, part_dest]
    arrived = lax.all_to_all(outgoing, "ch", split_axis=1, concat_axis=1, tiled=True)
    a_eta = arrived[0].reshape(width, width)
    b_gamma = arrived[1].reshape(width, width)

    perm = [(q, (q % n_chan) * n_rows + q // n_chan) for q in range(n_total)]
    coefs = lax.ppermute(
        jnp.concatenate([ph_factor.astype(f32), recouple], axis=0), ("ch", "row"), perm
    )
    weight = coefs[0].astype(bf16)[None, :]
    coef = coefs[1]

    ph_t = jnp.dot(a_eta * weight, b_gamma, preferred_element_type=f32)
    ph_t = ph_t - jnp.dot(b_gamma * weight, a_eta, preferred_element_type=f32)
    term_t = (ph_t * coef[:, None]).astype(bf16)
    ladder_in, _ = lax.optimization_barrier((ladder_in, term_t))
    sign = jnp.array([-1, 1], bf16)[:, None, None]
    own = lax.dynamic_index_in_dim(stacked, level, 1, False)
    own = jnp.roll(own, -level * rows, axis=-1)
    grid = [[None] * n_rows for _ in range(n_rows)]
    for d in range(n_rows):
        grid[0][d] = own[..., d * rows : (d + 1) * rows]
    for d in range(1, n_rows):
        piece = ladder_in[n_rows - d - 1]
        succ = d % (n_rows - 1) + 1
        grid[d][0] = sign * jnp.swapaxes(grid[0][d], -1, -2)
        grid[d][d] = piece[..., :rows]
        grid[d][succ] = piece[..., rows:]
        grid[succ][d] = sign * jnp.swapaxes(piece[..., rows:], -1, -2)
    whole = jnp.concatenate([jnp.concatenate(line, axis=-1) for line in grid], axis=-2)
    factor = lax.dynamic_index_in_dim(pp_factor, level, 0, False).astype(bf16)
    factor = jnp.roll(factor, -level * rows)
    left = jnp.concatenate([whole[0] * factor, whole[1] * factor], axis=-1)
    right = jnp.concatenate([whole[1], whole[0]], axis=-1)
    ladder_c = lax.dot_general(
        left, right, (((1,), (1,)), ((), ())), preferred_element_type=f32
    ).reshape(n_rows, rows, width)
    sending = jnp.stack([skip_block(ladder_c[a], a, rows) for a in range(n_rows)])
    returning = term_t.reshape(n_chan, slab, n_rows, rows).transpose(0, 2, 1, 3)
    landed = lax.all_to_all(
        returning.reshape(n_chan * n_rows, slab, rows),
        ("ch", "row"),
        split_axis=0,
        concat_axis=0,
        tiled=True,
    )
    landed = landed.reshape(n_chan, n_rows, slab, rows).transpose(1, 0, 2, 3)
    landed = landed.reshape(n_chan, ch_dev, slab, rows)
    returned = [sending[0]]
    for shift in range(1, n_rows):
        pairs = [(a, (a + shift) % n_rows) for a in range(n_rows)]
        returned.append(lax.ppermute(sending[shift], "row", pairs))
    sources = (level - jnp.arange(n_rows, dtype=jnp.int32)) % n_rows
    ladder = jnp.stack(returned)[sources]
    chosen = src_slot[:, mine].reshape(n_chan, ch_dev)
    onehot = (chosen[:, :, None] == jnp.arange(ch_dev, dtype=jnp.int32)[None, None, :]).astype(bf16)
    back = jnp.einsum("gts,gtwi->sigw", onehot, landed, preferred_element_type=f32)
    back = back.reshape(ch_dev, rows, width)

    local_d = pp_factor.astype(bf16)[:, None, :]
    left = jnp.concatenate([eta_pp * local_d, gamma_pp * local_d], axis=-1)
    right = jnp.concatenate([gamma_pp, eta_pp], axis=-1)
    diag = jnp.einsum("sik,sjk->sij", left, right, preferred_element_type=f32)
    ladder = jnp.concatenate([ladder, diag], axis=-1)
    ladder = jnp.roll(ladder, (level + 1) * rows, axis=-1)
    return (ladder + back).astype(bf16)


def solution(mesh):
    placed = (
        P("ch", "row", None),
        P("ch", "row", None),
        P("ch", None),
        P(("ch", "row"), None),
        P(("ch", "row"), None),
        P(),
    )
    return jax.shard_map(
        per_device, mesh=mesh, in_specs=placed, out_specs=P("ch", "row", None), check_vma=False
    )
```

```python
import jax
import jax.numpy as jnp
from jax import lax
from jax.sharding import PartitionSpec as P


def skip_block(x, b, size):
    return jnp.concatenate([x[..., (b + 1) * size :], x[..., : b * size]], axis=-1)


def per_device(eta_pp, gamma_pp, pp_factor, ph_factor, recouple, src_slot):
    f32 = jnp.float32
    bf16 = jnp.bfloat16
    n_chan = lax.axis_size("ch")
    n_rows = lax.axis_size("row")
    ch_dev, rows, width = eta_pp.shape
    slab = width // n_chan
    n_total = ch_dev * n_chan
    assert ch_dev == n_rows and rows % slab == 0 and n_chan * slab == width
    mine = lax.axis_index("ch")
    level = lax.axis_index("row")

    assert n_rows == 4
    stacked = jnp.stack([eta_pp, gamma_pp])
    upper = jnp.arange(rows)[:, None] < jnp.arange(rows)[None, :]
    lower = jnp.arange(rows)[:, None] > jnp.arange(rows)[None, :]
    ladder_in = []
    for shift in range(1, n_rows):
        block = lax.dynamic_index_in_dim(stacked, (level + shift) % n_rows, 1, False)
        d = n_rows - shift
        hop = (d % (n_rows - 1) + 1 - d) % n_rows
        own_blk = lax.dynamic_slice_in_dim(block, level * rows, rows, axis=-1)
        next_blk = lax.dynamic_slice_in_dim(
            block, ((level + hop) % n_rows) * rows, rows, axis=-1
        )
        packed = jnp.where(upper, own_blk[0], own_blk[1])
        pairs = [(a, (a + shift) % n_rows) for a in range(n_rows)]
        ladder_in.append(
            lax.ppermute(jnp.concatenate([packed[None], next_blk]), "row", pairs)
        )
    dest = jnp.arange(n_chan, dtype=jnp.int32)
    q_dest = level * n_chan + dest
    slot_dest = src_slot[q_dest, mine]
    part_dest = q_dest // ch_dev - level * (rows // slab)
    five = stacked.reshape(2, ch_dev, rows // slab, slab, width)
    outgoing = five[:, slot_dest, part_dest]
    arrived = lax.all_to_all(outgoing, "ch", split_axis=1, concat_axis=1, tiled=True)
    a_eta = arrived[0].reshape(width, width)
    b_gamma = arrived[1].reshape(width, width)

    perm = [(q, (q % n_chan) * n_rows + q // n_chan) for q in range(n_total)]
    coefs = lax.ppermute(
        jnp.concatenate([ph_factor.astype(f32), recouple], axis=0), ("ch", "row"), perm
    )
    weight = coefs[0].astype(bf16)[None, :]
    coef = coefs[1]

    ph_t = jnp.dot(a_eta * weight, b_gamma, preferred_element_type=f32)
    ph_t = ph_t - jnp.dot(b_gamma * weight, a_eta, preferred_element_type=f32)
    term_t = (ph_t * coef[:, None]).astype(bf16)
    ladder_in, _ = lax.optimization_barrier((ladder_in, term_t))
    sign = jnp.array([-1, 1], bf16)[:, None, None]
    own = lax.dynamic_index_in_dim(stacked, level, 1, False)
    own = jnp.roll(own, -level * rows, axis=-1)
    grid = [[None] * n_rows for _ in range(n_rows)]
    for d in range(n_rows):
        grid[0][d] = own[..., d * rows : (d + 1) * rows]
    for d in range(1, n_rows):
        piece = ladder_in[n_rows - d - 1]
        succ = d % (n_rows - 1) + 1
        grid[d][0] = sign * jnp.swapaxes(grid[0][d], -1, -2)
        packed = piece[0]
        eta_d = jnp.where(upper, packed, jnp.where(lower, -packed.T, jnp.zeros_like(packed)))
        gamma_d = jnp.where(lower | upper, jnp.where(upper, packed.T, packed), packed)
        grid[d][d] = jnp.stack([eta_d, gamma_d])
        grid[d][succ] = piece[1:]
        grid[succ][d] = sign * jnp.swapaxes(piece[1:], -1, -2)
    whole = jnp.concatenate([jnp.concatenate(line, axis=-1) for line in grid], axis=-2)
    factor = lax.dynamic_index_in_dim(pp_factor, level, 0, False).astype(bf16)
    factor = jnp.roll(factor, -level * rows)
    left = jnp.concatenate([whole[0] * factor, whole[1] * factor], axis=-1)
    right = jnp.concatenate([whole[1], whole[0]], axis=-1)
    ladder_c = lax.dot_general(
        left, right, (((1,), (1,)), ((), ())), preferred_element_type=f32
    ).reshape(n_rows, rows, width)
    sending = jnp.stack([skip_block(ladder_c[a], a, rows) for a in range(n_rows)])
    returning = term_t.reshape(n_chan, slab, n_rows, rows).transpose(0, 2, 1, 3)
    landed = lax.all_to_all(
        returning.reshape(n_chan * n_rows, slab, rows),
        ("ch", "row"),
        split_axis=0,
        concat_axis=0,
        tiled=True,
    )
    landed = landed.reshape(n_chan, n_rows, slab, rows).transpose(1, 0, 2, 3)
    landed = landed.reshape(n_chan, ch_dev, slab, rows)
    returned = [sending[0]]
    for shift in range(1, n_rows):
        pairs = [(a, (a + shift) % n_rows) for a in range(n_rows)]
        returned.append(lax.ppermute(sending[shift], "row", pairs))
    sources = (level - jnp.arange(n_rows, dtype=jnp.int32)) % n_rows
    ladder = jnp.stack(returned)[sources]
    chosen = src_slot[:, mine].reshape(n_chan, ch_dev)
    onehot = (chosen[:, :, None] == jnp.arange(ch_dev, dtype=jnp.int32)[None, None, :]).astype(bf16)
    back = jnp.einsum("gts,gtwi->sigw", onehot, landed, preferred_element_type=f32)
    back = back.reshape(ch_dev, rows, width)

    local_d = pp_factor.astype(bf16)[:, None, :]
    left = jnp.concatenate([eta_pp * local_d, gamma_pp * local_d], axis=-1)
    right = jnp.concatenate([gamma_pp, eta_pp], axis=-1)
    diag = jnp.einsum("sik,sjk->sij", left, right, preferred_element_type=f32)
    ladder = jnp.concatenate([ladder, diag], axis=-1)
    ladder = jnp.roll(ladder, (level + 1) * rows, axis=-1)
    return (ladder + back).astype(bf16)


def solution(mesh):
    placed = (
        P("ch", "row", None),
        P("ch", "row", None),
        P("ch", None),
        P(("ch", "row"), None),
        P(("ch", "row"), None),
        P(),
    )
    return jax.shard_map(
        per_device, mesh=mesh, in_specs=placed, out_specs=P("ch", "row", None), check_vma=False
    )
```

```python
import jax
import jax.numpy as jnp
from jax import lax
from jax.sharding import PartitionSpec as P


def skip_block(x, b, size):
    return jnp.concatenate([x[..., (b + 1) * size :], x[..., : b * size]], axis=-1)


def per_device(eta_pp, gamma_pp, pp_factor, ph_factor, recouple, src_slot):
    f32 = jnp.float32
    bf16 = jnp.bfloat16
    n_chan = lax.axis_size("ch")
    n_rows = lax.axis_size("row")
    ch_dev, rows, width = eta_pp.shape
    slab = width // n_chan
    n_total = ch_dev * n_chan
    assert ch_dev == n_rows and rows % slab == 0 and n_chan * slab == width
    mine = lax.axis_index("ch")
    level = lax.axis_index("row")

    assert n_rows == 4
    stacked = jnp.stack([eta_pp, gamma_pp])
    ladder_in = []
    for shift in range(1, n_rows):
        block = lax.dynamic_index_in_dim(stacked, (level + shift) % n_rows, 1, False)
        d = n_rows - shift
        hop = (d % (n_rows - 1) + 1 - d) % n_rows
        own_blk = lax.dynamic_slice_in_dim(block, level * rows, rows, axis=-1)
        next_blk = lax.dynamic_slice_in_dim(
            block, ((level + hop) % n_rows) * rows, rows, axis=-1
        )
        pairs = [(a, (a + shift) % n_rows) for a in range(n_rows)]
        ladder_in.append(
            lax.ppermute(jnp.concatenate([own_blk, next_blk], axis=-1), "row", pairs)
        )
    dest = jnp.arange(n_chan, dtype=jnp.int32)
    q_dest = level * n_chan + dest
    slot_dest = src_slot[q_dest, mine]
    part_dest = q_dest // ch_dev - level * (rows // slab)
    five = stacked.reshape(2, ch_dev, rows // slab, slab, width)
    outgoing = five[:, slot_dest, part_dest]
    arrived = lax.all_to_all(outgoing, "ch", split_axis=1, concat_axis=1, tiled=True)

    sign = jnp.array([-1, 1], bf16)[:, None, None]
    own = lax.dynamic_index_in_dim(stacked, level, 1, False)
    own = jnp.roll(own, -level * rows, axis=-1)
    grid = [[None] * n_rows for _ in range(n_rows)]
    for d in range(n_rows):
        grid[0][d] = own[..., d * rows : (d + 1) * rows]
    for d in range(1, n_rows):
        piece = ladder_in[n_rows - d - 1]
        succ = d % (n_rows - 1) + 1
        grid[d][0] = sign * jnp.swapaxes(grid[0][d], -1, -2)
        grid[d][d] = piece[..., :rows]
        grid[d][succ] = piece[..., rows:]
        grid[succ][d] = sign * jnp.swapaxes(piece[..., rows:], -1, -2)
    whole = jnp.concatenate([jnp.concatenate(line, axis=-1) for line in grid], axis=-2)
    factor = lax.dynamic_index_in_dim(pp_factor, level, 0, False).astype(bf16)
    factor = jnp.roll(factor, -level * rows)
    left = jnp.concatenate([whole[0] * factor, whole[1] * factor], axis=-1)
    right = jnp.concatenate([whole[1], whole[0]], axis=-1)
    ladder_c = lax.dot_general(
        left, right, (((1,), (1,)), ((), ())), preferred_element_type=f32
    ).reshape(n_rows, rows, width)
    sending = jnp.stack([skip_block(ladder_c[a], a, rows) for a in range(n_rows)])
    sending, arrived = lax.optimization_barrier((sending, arrived))
    returned = [sending[0]]
    for shift in range(1, n_rows):
        pairs = [(a, (a + shift) % n_rows) for a in range(n_rows)]
        returned.append(lax.ppermute(sending[shift], "row", pairs))
    sources = (level - jnp.arange(n_rows, dtype=jnp.int32)) % n_rows
    ladder = jnp.stack(returned)[sources]
    a_eta = arrived[0].reshape(width, width)
    b_gamma = arrived[1].reshape(width, width)
    perm = [(q, (q % n_chan) * n_rows + q // n_chan) for q in range(n_total)]
    coefs = lax.ppermute(
        jnp.concatenate([ph_factor.astype(f32), recouple], axis=0), ("ch", "row"), perm
    )
    weight = coefs[0].astype(bf16)[None, :]
    coef = coefs[1]

    ph_t = jnp.dot(a_eta * weight, b_gamma, preferred_element_type=f32)
    ph_t = ph_t - jnp.dot(b_gamma * weight, a_eta, preferred_element_type=f32)
    term_t = (ph_t * coef[:, None]).astype(bf16)
    returning = term_t.reshape(n_chan, slab, n_rows, rows).transpose(0, 2, 1, 3)
    landed = lax.all_to_all(
        returning.reshape(n_chan * n_rows, slab, rows),
        ("ch", "row"),
        split_axis=0,
        concat_axis=0,
        tiled=True,
    )
    landed = landed.reshape(n_chan, n_rows, slab, rows).transpose(1, 0, 2, 3)
    landed = landed.reshape(n_chan, ch_dev, slab, rows)
    chosen = src_slot[:, mine].reshape(n_chan, ch_dev)
    onehot = (chosen[:, :, None] == jnp.arange(ch_dev, dtype=jnp.int32)[None, None, :]).astype(bf16)
    back = jnp.einsum("gts,gtwi->sigw", onehot, landed, preferred_element_type=f32)
    back = back.reshape(ch_dev, rows, width)

    local_d = pp_factor.astype(bf16)[:, None, :]
    left = jnp.concatenate([eta_pp * local_d, gamma_pp * local_d], axis=-1)
    right = jnp.concatenate([gamma_pp, eta_pp], axis=-1)
    diag = jnp.einsum("sik,sjk->sij", left, right, preferred_element_type=f32)
    ladder = jnp.concatenate([ladder, diag], axis=-1)
    ladder = jnp.roll(ladder, (level + 1) * rows, axis=-1)
    return (ladder + back).astype(bf16)


def solution(mesh):
    placed = (
        P("ch", "row", None),
        P("ch", "row", None),
        P("ch", None),
        P(("ch", "row"), None),
        P(("ch", "row"), None),
        P(),
    )
    return jax.shard_map(
        per_device, mesh=mesh, in_specs=placed, out_specs=P("ch", "row", None), check_vma=False
    )
```

```python
import jax
import jax.numpy as jnp
from jax import lax
from jax.sharding import PartitionSpec as P


def skip_block(x, b, size):
    return jnp.concatenate([x[..., (b + 1) * size :], x[..., : b * size]], axis=-1)


def per_device(eta_pp, gamma_pp, pp_factor, ph_factor, recouple, src_slot):
    f32 = jnp.float32
    bf16 = jnp.bfloat16
    n_chan = lax.axis_size("ch")
    n_rows = lax.axis_size("row")
    ch_dev, rows, width = eta_pp.shape
    slab = width // n_chan
    n_total = ch_dev * n_chan
    assert ch_dev == n_rows and rows % slab == 0 and n_chan * slab == width
    mine = lax.axis_index("ch")
    level = lax.axis_index("row")

    assert n_rows == 4
    pair = lambda f: jnp.stack([f(eta_pp), f(gamma_pp)])
    ladder_in = []
    for shift in range(1, n_rows):
        block = pair(lambda x: lax.dynamic_index_in_dim(x, (level + shift) % n_rows, 0, False))
        d = n_rows - shift
        hop = (d % (n_rows - 1) + 1 - d) % n_rows
        own_blk = lax.dynamic_slice_in_dim(block, level * rows, rows, axis=-1)
        next_blk = lax.dynamic_slice_in_dim(
            block, ((level + hop) % n_rows) * rows, rows, axis=-1
        )
        pairs = [(a, (a + shift) % n_rows) for a in range(n_rows)]
        ladder_in.append(
            lax.ppermute(jnp.concatenate([own_blk, next_blk], axis=-1), "row", pairs)
        )
    dest = jnp.arange(n_chan, dtype=jnp.int32)
    q_dest = level * n_chan + dest
    slot_dest = src_slot[q_dest, mine]
    part_dest = q_dest // ch_dev - level * (rows // slab)
    outgoing = pair(lambda x: x.reshape(ch_dev, rows // slab, slab, width)[slot_dest, part_dest])
    arrived = lax.all_to_all(outgoing, "ch", split_axis=1, concat_axis=1, tiled=True)
    a_eta = arrived[0].reshape(width, width)
    b_gamma = arrived[1].reshape(width, width)

    perm = [(q, (q % n_chan) * n_rows + q // n_chan) for q in range(n_total)]
    coefs = lax.ppermute(
        jnp.concatenate([ph_factor.astype(f32), recouple], axis=0), ("ch", "row"), perm
    )
    weight = coefs[0].astype(bf16)[None, :]
    coef = coefs[1]

    ph_t = jnp.dot(a_eta * weight, b_gamma, preferred_element_type=f32)
    ph_t = ph_t - jnp.dot(b_gamma * weight, a_eta, preferred_element_type=f32)
    term_t = (ph_t * coef[:, None]).astype(bf16)
    ladder_in, _ = lax.optimization_barrier((ladder_in, term_t))
    sign = jnp.array([-1, 1], bf16)[:, None, None]
    own = pair(lambda x: lax.dynamic_index_in_dim(x, level, 0, False))
    own = jnp.roll(own, -level * rows, axis=-1)
    grid = [[None] * n_rows for _ in range(n_rows)]
    for d in range(n_rows):
        grid[0][d] = own[..., d * rows : (d + 1) * rows]
    for d in range(1, n_rows):
        piece = ladder_in[n_rows - d - 1]
        succ = d % (n_rows - 1) + 1
        grid[d][0] = sign * jnp.swapaxes(grid[0][d], -1, -2)
        grid[d][d] = piece[..., :rows]
        grid[d][succ] = piece[..., rows:]
        grid[succ][d] = sign * jnp.swapaxes(piece[..., rows:], -1, -2)
    whole = jnp.concatenate([jnp.concatenate(line, axis=-1) for line in grid], axis=-2)
    factor = lax.dynamic_index_in_dim(pp_factor, level, 0, False).astype(bf16)
    factor = jnp.roll(factor, -level * rows)
    left = jnp.concatenate([whole[0] * factor, whole[1] * factor], axis=-1)
    right = jnp.concatenate([whole[1], whole[0]], axis=-1)
    ladder_c = lax.dot_general(
        left, right, (((1,), (1,)), ((), ())), preferred_element_type=f32
    ).reshape(n_rows, rows, width)
    sending = jnp.stack([skip_block(ladder_c[a], a, rows) for a in range(n_rows)])
    returning = term_t.reshape(n_chan, slab, n_rows, rows).transpose(0, 2, 1, 3)
    landed = lax.all_to_all(
        returning.reshape(n_chan * n_rows, slab, rows),
        ("ch", "row"),
        split_axis=0,
        concat_axis=0,
        tiled=True,
    )
    landed = landed.reshape(n_chan, n_rows, slab, rows).transpose(1, 0, 2, 3)
    landed = landed.reshape(n_chan, ch_dev, slab, rows)
    returned = [sending[0]]
    for shift in range(1, n_rows):
        pairs = [(a, (a + shift) % n_rows) for a in range(n_rows)]
        returned.append(lax.ppermute(sending[shift], "row", pairs))
    sources = (level - jnp.arange(n_rows, dtype=jnp.int32)) % n_rows
    ladder = jnp.stack(returned)[sources]
    chosen = src_slot[:, mine].reshape(n_chan, ch_dev)
    onehot = (chosen[:, :, None] == jnp.arange(ch_dev, dtype=jnp.int32)[None, None, :]).astype(bf16)
    back = jnp.einsum("gts,gtwi->sigw", onehot, landed, preferred_element_type=f32)
    back = back.reshape(ch_dev, rows, width)

    local_d = pp_factor.astype(bf16)[:, None, :]
    left = jnp.concatenate([eta_pp * local_d, gamma_pp * local_d], axis=-1)
    right = jnp.concatenate([gamma_pp, eta_pp], axis=-1)
    diag = jnp.einsum("sik,sjk->sij", left, right, preferred_element_type=f32)
    ladder = jnp.concatenate([ladder, diag], axis=-1)
    ladder = jnp.roll(ladder, (level + 1) * rows, axis=-1)
    return (ladder + back).astype(bf16)


def solution(mesh):
    placed = (
        P("ch", "row", None),
        P("ch", "row", None),
        P("ch", None),
        P(("ch", "row"), None),
        P(("ch", "row"), None),
        P(),
    )
    return jax.shard_map(
        per_device, mesh=mesh, in_specs=placed, out_specs=P("ch", "row", None), check_vma=False
    )
```

```python
import jax
import jax.numpy as jnp
from jax import lax
from jax.sharding import PartitionSpec as P


def skip_block(x, b, size):
    return jnp.concatenate([x[..., (b + 1) * size :], x[..., : b * size]], axis=-1)


def per_device(eta_pp, gamma_pp, pp_factor, ph_factor, recouple, src_slot):
    f32 = jnp.float32
    bf16 = jnp.bfloat16
    n_chan = lax.axis_size("ch")
    n_rows = lax.axis_size("row")
    ch_dev, rows, width = eta_pp.shape
    slab = width // n_chan
    n_total = ch_dev * n_chan
    assert ch_dev == n_rows and rows % slab == 0 and n_chan * slab == width
    mine = lax.axis_index("ch")
    level = lax.axis_index("row")

    assert n_rows == 4
    pair = lambda f: jnp.stack([f(eta_pp), f(gamma_pp)])
    ladder_in = []
    for shift in range(1, n_rows):
        block = pair(lambda x: lax.dynamic_index_in_dim(x, (level + shift) % n_rows, 0, False))
        d = n_rows - shift
        hop = (d % (n_rows - 1) + 1 - d) % n_rows
        own_blk = lax.dynamic_slice_in_dim(block, level * rows, rows, axis=-1)
        next_blk = lax.dynamic_slice_in_dim(
            block, ((level + hop) % n_rows) * rows, rows, axis=-1
        )
        pairs = [(a, (a + shift) % n_rows) for a in range(n_rows)]
        ladder_in.append(
            lax.ppermute(jnp.concatenate([own_blk, next_blk], axis=-1), "row", pairs)
        )
    dest = jnp.arange(n_chan, dtype=jnp.int32)
    q_dest = level * n_chan + dest
    slot_dest = src_slot[q_dest, mine]
    part_dest = q_dest // ch_dev - level * (rows // slab)
    outgoing = pair(lambda x: x.reshape(ch_dev, rows // slab, slab, width)[slot_dest, part_dest])
    arrived = lax.all_to_all(outgoing, "ch", split_axis=1, concat_axis=1, tiled=True)
    a_eta = arrived[0].reshape(width, width)
    b_gamma = arrived[1].reshape(width, width)

    perm = [(q, (q % n_chan) * n_rows + q // n_chan) for q in range(n_total)]
    coefs = lax.ppermute(
        jnp.concatenate([ph_factor.astype(f32), recouple], axis=0), ("ch", "row"), perm
    )
    weight = coefs[0].astype(bf16)[None, :]
    coef = coefs[1]

    split = lambda x: x.reshape(n_chan, slab, width)
    cols = lambda x: x.reshape(width, n_rows, rows)
    ph_t = jnp.einsum(
        "ewk,kri->erwi", split(a_eta * weight), cols(b_gamma), preferred_element_type=f32
    )
    ph_t = ph_t - jnp.einsum(
        "ewk,kri->erwi", split(b_gamma * weight), cols(a_eta), preferred_element_type=f32
    )
    term_t = (ph_t * coef.reshape(n_chan, 1, slab, 1)).astype(bf16)
    ladder_in, _ = lax.optimization_barrier((ladder_in, term_t))
    sign = jnp.array([-1, 1], bf16)[:, None, None]
    own = pair(lambda x: lax.dynamic_index_in_dim(x, level, 0, False))
    own = jnp.roll(own, -level * rows, axis=-1)
    grid = [[None] * n_rows for _ in range(n_rows)]
    for d in range(n_rows):
        grid[0][d] = own[..., d * rows : (d + 1) * rows]
    for d in range(1, n_rows):
        piece = ladder_in[n_rows - d - 1]
        succ = d % (n_rows - 1) + 1
        grid[d][0] = sign * jnp.swapaxes(grid[0][d], -1, -2)
        grid[d][d] = piece[..., :rows]
        grid[d][succ] = piece[..., rows:]
        grid[succ][d] = sign * jnp.swapaxes(piece[..., rows:], -1, -2)
    whole = jnp.concatenate([jnp.concatenate(line, axis=-1) for line in grid], axis=-2)
    factor = lax.dynamic_index_in_dim(pp_factor, level, 0, False).astype(bf16)
    factor = jnp.roll(factor, -level * rows)
    left = jnp.concatenate([whole[0] * factor, whole[1] * factor], axis=-1)
    right = jnp.concatenate([whole[1], whole[0]], axis=-1)
    ladder_c = lax.dot_general(
        left, right, (((1,), (1,)), ((), ())), preferred_element_type=f32
    ).reshape(n_rows, rows, width)
    sending = jnp.stack([skip_block(ladder_c[a], a, rows) for a in range(n_rows)])
    returning = term_t
    landed = lax.all_to_all(
        returning.reshape(n_chan * n_rows, slab, rows),
        ("ch", "row"),
        split_axis=0,
        concat_axis=0,
        tiled=True,
    )
    landed = landed.reshape(n_chan, n_rows, slab, rows).transpose(1, 0, 2, 3)
    landed = landed.reshape(n_chan, ch_dev, slab, rows)
    returned = [sending[0]]
    for shift in range(1, n_rows):
        pairs = [(a, (a + shift) % n_rows) for a in range(n_rows)]
        returned.append(lax.ppermute(sending[shift], "row", pairs))
    ladder = jnp.stack(
        [lax.select_n((level - s) % n_rows, *returned) for s in range(n_rows)]
    )
    chosen = src_slot[:, mine].reshape(n_chan, ch_dev)
    onehot = (chosen[:, :, None] == jnp.arange(ch_dev, dtype=jnp.int32)[None, None, :]).astype(bf16)
    back = jnp.einsum("gts,gtwi->sigw", onehot, landed, preferred_element_type=f32)
    back = back.reshape(ch_dev, rows, width)

    local_d = pp_factor.astype(bf16)[:, None, :]
    left = jnp.concatenate([eta_pp * local_d, gamma_pp * local_d], axis=-1)
    right = jnp.concatenate([gamma_pp, eta_pp], axis=-1)
    diag = jnp.einsum("sik,sjk->sij", left, right, preferred_element_type=f32)
    ladder = jnp.concatenate([ladder, diag], axis=-1)
    ladder = jnp.roll(ladder, (level + 1) * rows, axis=-1)
    return (ladder + back).astype(bf16)


def solution(mesh):
    placed = (
        P("ch", "row", None),
        P("ch", "row", None),
        P("ch", None),
        P(("ch", "row"), None),
        P(("ch", "row"), None),
        P(),
    )
    return jax.shard_map(
        per_device, mesh=mesh, in_specs=placed, out_specs=P("ch", "row", None), check_vma=False
    )
```

```python
import jax
import jax.numpy as jnp
from jax import lax
from jax.sharding import PartitionSpec as P


def skip_block(x, b, size):
    return jnp.concatenate([x[..., (b + 1) * size :], x[..., : b * size]], axis=-1)


def per_device(eta_pp, gamma_pp, pp_factor, ph_factor, recouple, src_slot):
    f32 = jnp.float32
    bf16 = jnp.bfloat16
    n_chan = lax.axis_size("ch")
    n_rows = lax.axis_size("row")
    ch_dev, rows, width = eta_pp.shape
    slab = width // n_chan
    n_total = ch_dev * n_chan
    assert ch_dev == n_rows and rows % slab == 0 and n_chan * slab == width
    mine = lax.axis_index("ch")
    level = lax.axis_index("row")

    assert n_rows == 4
    pair = lambda f: jnp.stack([f(eta_pp), f(gamma_pp)])
    ladder_in = []
    for shift in range(1, n_rows):
        block = pair(lambda x: lax.dynamic_index_in_dim(x, (level + shift) % n_rows, 0, False))
        d = n_rows - shift
        hop = (d % (n_rows - 1) + 1 - d) % n_rows
        own_blk = lax.dynamic_slice_in_dim(block, level * rows, rows, axis=-1)
        next_blk = lax.dynamic_slice_in_dim(
            block, ((level + hop) % n_rows) * rows, rows, axis=-1
        )
        pairs = [(a, (a + shift) % n_rows) for a in range(n_rows)]
        ladder_in.append(
            lax.ppermute(jnp.concatenate([own_blk, next_blk], axis=-1), "row", pairs)
        )
    dest = jnp.arange(n_chan, dtype=jnp.int32)
    q_dest = level * n_chan + dest
    slot_dest = src_slot[q_dest, mine]
    part_dest = q_dest // ch_dev - level * (rows // slab)
    outgoing = pair(lambda x: x.reshape(ch_dev, rows // slab, slab, width)[slot_dest, part_dest])
    arrived = lax.all_to_all(outgoing, "ch", split_axis=1, concat_axis=1, tiled=True)
    a_eta = arrived[0].reshape(width, width)
    b_gamma = arrived[1].reshape(width, width)

    perm = [(q, (q % n_chan) * n_rows + q // n_chan) for q in range(n_total)]
    coefs = lax.ppermute(
        jnp.concatenate([ph_factor.astype(f32), recouple], axis=0), ("ch", "row"), perm
    )
    weight = coefs[0].astype(bf16)[None, :]
    coef = coefs[1]

    ph_t = jnp.dot(a_eta * weight, b_gamma, preferred_element_type=f32)
    ph_t = ph_t - jnp.dot(b_gamma * weight, a_eta, preferred_element_type=f32)
    term_t = (ph_t * coef[:, None]).astype(bf16)
    ladder_in, _ = lax.optimization_barrier((ladder_in, term_t))
    sign = jnp.array([-1, 1], bf16)[:, None, None]
    own = pair(lambda x: lax.dynamic_index_in_dim(x, level, 0, False))
    own = jnp.roll(own, -level * rows, axis=-1)
    grid = [[None] * n_rows for _ in range(n_rows)]
    for d in range(n_rows):
        grid[0][d] = own[..., d * rows : (d + 1) * rows]
    for d in range(1, n_rows):
        piece = ladder_in[n_rows - d - 1]
        succ = d % (n_rows - 1) + 1
        grid[d][0] = sign * jnp.swapaxes(grid[0][d], -1, -2)
        grid[d][d] = piece[..., :rows]
        grid[d][succ] = piece[..., rows:]
        grid[succ][d] = sign * jnp.swapaxes(piece[..., rows:], -1, -2)
    whole = jnp.concatenate([jnp.concatenate(line, axis=-1) for line in grid], axis=-2)
    factor = lax.dynamic_index_in_dim(pp_factor, level, 0, False).astype(bf16)
    factor = jnp.roll(factor, -level * rows)
    left = jnp.concatenate([whole[0] * factor, whole[1] * factor], axis=-1)
    right = jnp.concatenate([whole[1], whole[0]], axis=-1)
    ladder_c = lax.dot_general(
        left, right, (((1,), (1,)), ((), ())), preferred_element_type=f32
    ).reshape(n_rows, rows, width)
    sending = jnp.stack([skip_block(ladder_c[a], a, rows) for a in range(n_rows)])
    returning = term_t.reshape(n_chan, slab, n_rows, rows).transpose(0, 2, 1, 3)
    landed = lax.all_to_all(
        returning.reshape(n_chan * n_rows, slab, rows),
        ("ch", "row"),
        split_axis=0,
        concat_axis=0,
        tiled=True,
    )
    landed = landed.reshape(n_chan, n_rows, slab, rows).transpose(1, 0, 2, 3)
    landed = landed.reshape(n_chan, ch_dev, slab, rows)
    returned = [sending[0]]
    for shift in range(1, n_rows):
        pairs = [(a, (a + shift) % n_rows) for a in range(n_rows)]
        returned.append(lax.ppermute(sending[shift], "row", pairs))
    ladder = jnp.stack(
        [lax.select_n((level - s) % n_rows, *returned) for s in range(n_rows)]
    )
    chosen = src_slot[:, mine].reshape(n_chan, ch_dev)
    onehot = (chosen[:, :, None] == jnp.arange(ch_dev, dtype=jnp.int32)[None, None, :]).astype(bf16)
    back = jnp.einsum("gts,gtwi->sigw", onehot, landed, preferred_element_type=f32)
    back = back.reshape(ch_dev, rows, width)

    local_d = pp_factor.astype(bf16)[:, None, :]
    left = jnp.concatenate([eta_pp * local_d, gamma_pp * local_d], axis=-1)
    right = jnp.concatenate([gamma_pp, eta_pp], axis=-1)
    diag = jnp.einsum("sik,sjk->sij", left, right, preferred_element_type=f32)
    ladder = jnp.concatenate([ladder, diag], axis=-1)
    ladder = jnp.roll(ladder, (level + 1) * rows, axis=-1)
    return (ladder + back).astype(bf16)


def solution(mesh):
    placed = (
        P("ch", "row", None),
        P("ch", "row", None),
        P("ch", None),
        P(("ch", "row"), None),
        P(("ch", "row"), None),
        P(),
    )
    return jax.shard_map(
        per_device, mesh=mesh, in_specs=placed, out_specs=P("ch", "row", None), check_vma=False
    )
```

```python
import jax
import jax.numpy as jnp
from jax import lax
from jax.sharding import PartitionSpec as P


def skip_block(x, b, size):
    return jnp.concatenate([x[..., (b + 1) * size :], x[..., : b * size]], axis=-1)


def per_device(eta_pp, gamma_pp, pp_factor, ph_factor, recouple, src_slot):
    f32 = jnp.float32
    bf16 = jnp.bfloat16
    n_chan = lax.axis_size("ch")
    n_rows = lax.axis_size("row")
    ch_dev, rows, width = eta_pp.shape
    slab = width // n_chan
    n_total = ch_dev * n_chan
    assert ch_dev == n_rows and rows % slab == 0 and n_chan * slab == width
    mine = lax.axis_index("ch")
    level = lax.axis_index("row")

    assert n_rows == 4
    pair = lambda f: jnp.stack([f(eta_pp), f(gamma_pp)])
    ladder_in = []
    for shift in range(1, n_rows):
        block = pair(lambda x: lax.dynamic_index_in_dim(x, (level + shift) % n_rows, 0, False))
        d = n_rows - shift
        hop = (d % (n_rows - 1) + 1 - d) % n_rows
        own_blk = lax.dynamic_slice_in_dim(block, level * rows, rows, axis=-1)
        next_blk = lax.dynamic_slice_in_dim(
            block, ((level + hop) % n_rows) * rows, rows, axis=-1
        )
        pairs = [(a, (a + shift) % n_rows) for a in range(n_rows)]
        ladder_in.append(
            lax.ppermute(jnp.concatenate([own_blk, next_blk], axis=-1), "row", pairs)
        )
    dest = jnp.arange(n_chan, dtype=jnp.int32)
    q_dest = level * n_chan + dest
    slot_dest = src_slot[q_dest, mine]
    part_dest = q_dest // ch_dev - level * (rows // slab)
    outgoing = pair(lambda x: x.reshape(ch_dev, rows // slab, slab, width)[slot_dest, part_dest])
    arrived = lax.all_to_all(outgoing, "ch", split_axis=1, concat_axis=1, tiled=True)

    sign = jnp.array([-1, 1], bf16)[:, None, None]
    own = pair(lambda x: lax.dynamic_index_in_dim(x, level, 0, False))
    own = jnp.roll(own, -level * rows, axis=-1)
    own_cols = [sign * jnp.swapaxes(own[..., d * rows : (d + 1) * rows], -1, -2) for d in range(1, n_rows)]
    factor = lax.dynamic_index_in_dim(pp_factor, level, 0, False).astype(bf16)
    factor = jnp.roll(factor, -level * rows)
    local_d = pp_factor.astype(bf16)[:, None, :]
    left = jnp.concatenate([eta_pp * local_d, gamma_pp * local_d], axis=-1)
    right = jnp.concatenate([gamma_pp, eta_pp], axis=-1)
    diag = jnp.einsum("sik,sjk->sij", left, right, preferred_element_type=f32)
    arrived, own, own_cols, factor, diag = lax.optimization_barrier(
        (arrived, own, own_cols, factor, diag)
    )
    a_eta = arrived[0].reshape(width, width)
    b_gamma = arrived[1].reshape(width, width)

    perm = [(q, (q % n_chan) * n_rows + q // n_chan) for q in range(n_total)]
    coefs = lax.ppermute(
        jnp.concatenate([ph_factor.astype(f32), recouple], axis=0), ("ch", "row"), perm
    )
    weight = coefs[0].astype(bf16)[None, :]
    coef = coefs[1]

    ph_t = jnp.dot(a_eta * weight, b_gamma, preferred_element_type=f32)
    ph_t = ph_t - jnp.dot(b_gamma * weight, a_eta, preferred_element_type=f32)
    term_t = (ph_t * coef[:, None]).astype(bf16)
    ladder_in, _ = lax.optimization_barrier((ladder_in, term_t))
    grid = [[None] * n_rows for _ in range(n_rows)]
    for d in range(n_rows):
        grid[0][d] = own[..., d * rows : (d + 1) * rows]
    for d in range(1, n_rows):
        piece = ladder_in[n_rows - d - 1]
        succ = d % (n_rows - 1) + 1
        grid[d][0] = own_cols[d - 1]
        grid[d][d] = piece[..., :rows]
        grid[d][succ] = piece[..., rows:]
        grid[succ][d] = sign * jnp.swapaxes(piece[..., rows:], -1, -2)
    whole = jnp.concatenate([jnp.concatenate(line, axis=-1) for line in grid], axis=-2)
    left = jnp.concatenate([whole[0] * factor, whole[1] * factor], axis=-1)
    right = jnp.concatenate([whole[1], whole[0]], axis=-1)
    ladder_c = lax.dot_general(
        left, right, (((1,), (1,)), ((), ())), preferred_element_type=f32
    ).reshape(n_rows, rows, width)
    sending = jnp.stack([skip_block(ladder_c[a], a, rows) for a in range(n_rows)])
    returning = term_t.reshape(n_chan, slab, n_rows, rows).transpose(0, 2, 1, 3)
    landed = lax.all_to_all(
        returning.reshape(n_chan * n_rows, slab, rows),
        ("ch", "row"),
        split_axis=0,
        concat_axis=0,
        tiled=True,
    )
    landed = landed.reshape(n_chan, n_rows, slab, rows).transpose(1, 0, 2, 3)
    landed = landed.reshape(n_chan, ch_dev, slab, rows)
    returned = [sending[0]]
    for shift in range(1, n_rows):
        pairs = [(a, (a + shift) % n_rows) for a in range(n_rows)]
        returned.append(lax.ppermute(sending[shift], "row", pairs))
    ladder = jnp.stack(
        [lax.select_n((level - s) % n_rows, *returned) for s in range(n_rows)]
    )
    chosen = src_slot[:, mine].reshape(n_chan, ch_dev)
    onehot = (chosen[:, :, None] == jnp.arange(ch_dev, dtype=jnp.int32)[None, None, :]).astype(bf16)
    back = jnp.einsum("gts,gtwi->sigw", onehot, landed, preferred_element_type=f32)
    back = back.reshape(ch_dev, rows, width)

    ladder = jnp.concatenate([ladder, diag], axis=-1)
    ladder = jnp.roll(ladder, (level + 1) * rows, axis=-1)
    return (ladder + back).astype(bf16)


def solution(mesh):
    placed = (
        P("ch", "row", None),
        P("ch", "row", None),
        P("ch", None),
        P(("ch", "row"), None),
        P(("ch", "row"), None),
        P(),
    )
    return jax.shard_map(
        per_device, mesh=mesh, in_specs=placed, out_specs=P("ch", "row", None), check_vma=False
    )
```

```python
import jax
import jax.numpy as jnp
from jax import lax
from jax.sharding import PartitionSpec as P


def skip_block(x, b, size):
    return jnp.concatenate([x[..., (b + 1) * size :], x[..., : b * size]], axis=-1)


def per_device(eta_pp, gamma_pp, pp_factor, ph_factor, recouple, src_slot):
    f32 = jnp.float32
    bf16 = jnp.bfloat16
    n_chan = lax.axis_size("ch")
    n_rows = lax.axis_size("row")
    ch_dev, rows, width = eta_pp.shape
    slab = width // n_chan
    n_total = ch_dev * n_chan
    assert ch_dev == n_rows and rows % slab == 0 and n_chan * slab == width
    mine = lax.axis_index("ch")
    level = lax.axis_index("row")

    assert n_rows == 4
    pair = lambda f: jnp.stack([f(eta_pp), f(gamma_pp)])
    ladder_in = []
    for shift in range(1, n_rows):
        block = pair(lambda x: lax.dynamic_index_in_dim(x, (level + shift) % n_rows, 0, False))
        d = n_rows - shift
        hop = (d % (n_rows - 1) + 1 - d) % n_rows
        own_blk = lax.dynamic_slice_in_dim(block, level * rows, rows, axis=-1)
        next_blk = lax.dynamic_slice_in_dim(
            block, ((level + hop) % n_rows) * rows, rows, axis=-1
        )
        pairs = [(a, (a + shift) % n_rows) for a in range(n_rows)]
        ladder_in.append(
            lax.ppermute(jnp.concatenate([own_blk, next_blk], axis=-1), "row", pairs)
        )
    dest = jnp.arange(n_chan, dtype=jnp.int32)
    q_dest = level * n_chan + dest
    slot_dest = src_slot[q_dest, mine]
    part_dest = q_dest // ch_dev - level * (rows // slab)
    outgoing = pair(lambda x: x.reshape(ch_dev, rows // slab, slab, width)[slot_dest, part_dest])
    arrived = lax.all_to_all(outgoing, "ch", split_axis=1, concat_axis=1, tiled=True)
    a_eta = arrived[0].reshape(width, width)
    b_gamma = arrived[1].reshape(width, width)

    perm = [(q, (q % n_chan) * n_rows + q // n_chan) for q in range(n_total)]
    coefs = lax.ppermute(
        jnp.concatenate([ph_factor.astype(f32), recouple], axis=0), ("ch", "row"), perm
    )
    weight = coefs[0].astype(bf16)[None, :]
    coef = coefs[1]

    ph_t = jnp.dot(a_eta * weight, b_gamma, preferred_element_type=f32)
    ph_t = ph_t - jnp.dot(b_gamma * weight, a_eta, preferred_element_type=f32)
    term_t = (ph_t * coef[:, None]).astype(bf16)
    ladder_in, _ = lax.optimization_barrier((ladder_in, term_t))
    sign = jnp.array([-1, 1], bf16)[:, None, None]
    own = pair(lambda x: lax.dynamic_index_in_dim(x, level, 0, False))
    own = jnp.roll(own, -level * rows, axis=-1)
    grid = [[None] * n_rows for _ in range(n_rows)]
    for d in range(n_rows):
        grid[0][d] = own[..., d * rows : (d + 1) * rows]
    for d in range(1, n_rows):
        piece = ladder_in[n_rows - d - 1]
        succ = d % (n_rows - 1) + 1
        grid[d][0] = sign * jnp.swapaxes(grid[0][d], -1, -2)
        grid[d][d] = piece[..., :rows]
        grid[d][succ] = piece[..., rows:]
        grid[succ][d] = sign * jnp.swapaxes(piece[..., rows:], -1, -2)
    whole = jnp.concatenate([jnp.concatenate(line, axis=-1) for line in grid], axis=-2)
    factor = lax.dynamic_index_in_dim(pp_factor, level, 0, False).astype(bf16)
    factor = jnp.roll(factor, -level * rows)
    left = jnp.concatenate([whole[0] * factor, whole[1] * factor], axis=-1)
    right = jnp.concatenate([whole[1], whole[0]], axis=-1)
    ladder_c = lax.dot_general(
        left, right, (((1,), (1,)), ((), ())), preferred_element_type=f32
    ).reshape(n_rows, rows, width)
    sending = jnp.stack([skip_block(ladder_c[a], a, rows) for a in range(n_rows)])
    returning = term_t.reshape(n_chan, slab, n_rows, rows).transpose(0, 2, 1, 3)
    landed = lax.all_to_all(
        returning.reshape(n_chan * n_rows, slab, rows),
        ("ch", "row"),
        split_axis=0,
        concat_axis=0,
        tiled=True,
    )
    landed = landed.reshape(n_chan, n_rows, slab, rows).transpose(1, 0, 2, 3)
    landed = landed.reshape(n_chan, ch_dev, slab, rows)
    returned = [sending[0]]
    for shift in range(1, n_rows):
        pairs = [(a, (a + shift) % n_rows) for a in range(n_rows)]
        returned.append(lax.ppermute(sending[shift], "row", pairs))
    ladder = jnp.stack(
        [lax.select_n((level - s) % n_rows, *returned) for s in range(n_rows)]
    )
    chosen = src_slot[:, mine].reshape(n_chan, ch_dev)
    picked = chosen[None, :, :] == jnp.arange(ch_dev, dtype=jnp.int32)[:, None, None]
    back = jnp.where(picked[..., None, None], landed[None].astype(f32), 0.0).sum(axis=2)
    back = back.transpose(0, 3, 1, 2).reshape(ch_dev, rows, width)

    local_d = pp_factor.astype(bf16)[:, None, :]
    left = jnp.concatenate([eta_pp * local_d, gamma_pp * local_d], axis=-1)
    right = jnp.concatenate([gamma_pp, eta_pp], axis=-1)
    diag = jnp.einsum("sik,sjk->sij", left, right, preferred_element_type=f32)
    ladder = jnp.concatenate([ladder, diag], axis=-1)
    ladder = jnp.roll(ladder, (level + 1) * rows, axis=-1)
    return (ladder + back).astype(bf16)


def solution(mesh):
    placed = (
        P("ch", "row", None),
        P("ch", "row", None),
        P("ch", None),
        P(("ch", "row"), None),
        P(("ch", "row"), None),
        P(),
    )
    return jax.shard_map(
        per_device, mesh=mesh, in_specs=placed, out_specs=P("ch", "row", None), check_vma=False
    )
```

```python
import jax
import jax.numpy as jnp
from jax import lax
from jax.experimental.layout import Layout, with_layout_constraint
from jax.sharding import PartitionSpec as P


def skip_block(x, b, size):
    return jnp.concatenate([x[..., (b + 1) * size :], x[..., : b * size]], axis=-1)


def per_device(eta_pp, gamma_pp, pp_factor, ph_factor, recouple, src_slot):
    f32 = jnp.float32
    bf16 = jnp.bfloat16
    n_chan = lax.axis_size("ch")
    n_rows = lax.axis_size("row")
    ch_dev, rows, width = eta_pp.shape
    slab = width // n_chan
    n_total = ch_dev * n_chan
    assert ch_dev == n_rows and rows % slab == 0 and n_chan * slab == width
    mine = lax.axis_index("ch")
    level = lax.axis_index("row")

    assert n_rows == 4
    pair = lambda f: jnp.stack([f(eta_pp), f(gamma_pp)])
    ladder_in = []
    for shift in range(1, n_rows):
        block = pair(lambda x: lax.dynamic_index_in_dim(x, (level + shift) % n_rows, 0, False))
        d = n_rows - shift
        hop = (d % (n_rows - 1) + 1 - d) % n_rows
        own_blk = lax.dynamic_slice_in_dim(block, level * rows, rows, axis=-1)
        next_blk = lax.dynamic_slice_in_dim(
            block, ((level + hop) % n_rows) * rows, rows, axis=-1
        )
        pairs = [(a, (a + shift) % n_rows) for a in range(n_rows)]
        ladder_in.append(
            lax.ppermute(jnp.concatenate([own_blk, next_blk], axis=-1), "row", pairs)
        )
    dest = jnp.arange(n_chan, dtype=jnp.int32)
    q_dest = level * n_chan + dest
    slot_dest = src_slot[q_dest, mine]
    part_dest = q_dest // ch_dev - level * (rows // slab)
    outgoing = pair(lambda x: x.reshape(ch_dev, rows // slab, slab, width)[slot_dest, part_dest])
    arrived = lax.all_to_all(outgoing, "ch", split_axis=1, concat_axis=1, tiled=True)
    a_eta = arrived[0].reshape(width, width)
    b_gamma = arrived[1].reshape(width, width)

    perm = [(q, (q % n_chan) * n_rows + q // n_chan) for q in range(n_total)]
    coefs = lax.ppermute(
        jnp.concatenate([ph_factor.astype(f32), recouple], axis=0), ("ch", "row"), perm
    )
    weight = coefs[0].astype(bf16)[None, :]
    coef = coefs[1]

    ph_t = jnp.dot(a_eta * weight, b_gamma, preferred_element_type=f32)
    ph_t = ph_t - jnp.dot(b_gamma * weight, a_eta, preferred_element_type=f32)
    term_t = (ph_t * coef[:, None]).astype(bf16)
    ladder_in, _ = lax.optimization_barrier((ladder_in, term_t))
    sign = jnp.array([-1, 1], bf16)[:, None, None]
    own = pair(lambda x: lax.dynamic_index_in_dim(x, level, 0, False))
    own = jnp.roll(own, -level * rows, axis=-1)
    grid = [[None] * n_rows for _ in range(n_rows)]
    for d in range(n_rows):
        grid[0][d] = own[..., d * rows : (d + 1) * rows]
    for d in range(1, n_rows):
        piece = ladder_in[n_rows - d - 1]
        succ = d % (n_rows - 1) + 1
        grid[d][0] = sign * jnp.swapaxes(grid[0][d], -1, -2)
        grid[d][d] = piece[..., :rows]
        grid[d][succ] = piece[..., rows:]
        grid[succ][d] = sign * jnp.swapaxes(piece[..., rows:], -1, -2)
    whole = jnp.concatenate([jnp.concatenate(line, axis=-1) for line in grid], axis=-2)
    factor = lax.dynamic_index_in_dim(pp_factor, level, 0, False).astype(bf16)
    factor = jnp.roll(factor, -level * rows)
    left = jnp.concatenate([whole[0] * factor, whole[1] * factor], axis=-1)
    right = jnp.concatenate([whole[1], whole[0]], axis=-1)
    ladder_c = lax.dot_general(
        left, right, (((1,), (1,)), ((), ())), preferred_element_type=f32
    )
    ladder_c = with_layout_constraint(ladder_c, Layout((0, 1))).reshape(n_rows, rows, width)
    sending = jnp.stack([skip_block(ladder_c[a], a, rows) for a in range(n_rows)])
    returning = term_t.reshape(n_chan, slab, n_rows, rows).transpose(0, 2, 1, 3)
    landed = lax.all_to_all(
        returning.reshape(n_chan * n_rows, slab, rows),
        ("ch", "row"),
        split_axis=0,
        concat_axis=0,
        tiled=True,
    )
    landed = landed.reshape(n_chan, n_rows, slab, rows).transpose(1, 0, 2, 3)
    landed = landed.reshape(n_chan, ch_dev, slab, rows)
    returned = [sending[0]]
    for shift in range(1, n_rows):
        pairs = [(a, (a + shift) % n_rows) for a in range(n_rows)]
        returned.append(lax.ppermute(sending[shift], "row", pairs))
    ladder = jnp.stack(
        [lax.select_n((level - s) % n_rows, *returned) for s in range(n_rows)]
    )
    chosen = src_slot[:, mine].reshape(n_chan, ch_dev)
    onehot = (chosen[:, :, None] == jnp.arange(ch_dev, dtype=jnp.int32)[None, None, :]).astype(bf16)
    back = jnp.einsum("gts,gtwi->sigw", onehot, landed, preferred_element_type=f32)
    back = back.reshape(ch_dev, rows, width)

    local_d = pp_factor.astype(bf16)[:, None, :]
    left = jnp.concatenate([eta_pp * local_d, gamma_pp * local_d], axis=-1)
    right = jnp.concatenate([gamma_pp, eta_pp], axis=-1)
    diag = jnp.einsum("sik,sjk->sij", left, right, preferred_element_type=f32)
    ladder = jnp.concatenate([ladder, diag], axis=-1)
    ladder = jnp.roll(ladder, (level + 1) * rows, axis=-1)
    return (ladder + back).astype(bf16)


def solution(mesh):
    placed = (
        P("ch", "row", None),
        P("ch", "row", None),
        P("ch", None),
        P(("ch", "row"), None),
        P(("ch", "row"), None),
        P(),
    )
    return jax.shard_map(
        per_device, mesh=mesh, in_specs=placed, out_specs=P("ch", "row", None), check_vma=False
    )
```

```python
import jax
import jax.numpy as jnp
from jax import lax
from jax.sharding import PartitionSpec as P


def skip_block(x, b, size):
    return jnp.concatenate([x[..., (b + 1) * size :], x[..., : b * size]], axis=-1)


def per_device(eta_pp, gamma_pp, pp_factor, ph_factor, recouple, src_slot):
    f32 = jnp.float32
    bf16 = jnp.bfloat16
    n_chan = lax.axis_size("ch")
    n_rows = lax.axis_size("row")
    ch_dev, rows, width = eta_pp.shape
    slab = width // n_chan
    n_total = ch_dev * n_chan
    assert ch_dev == n_rows and rows % slab == 0 and n_chan * slab == width
    mine = lax.axis_index("ch")
    level = lax.axis_index("row")

    assert n_rows == 4
    pair = lambda f: jnp.stack([f(eta_pp), f(gamma_pp)])
    ladder_in = []
    for shift in range(1, n_rows):
        block = pair(lambda x: lax.dynamic_index_in_dim(x, (level + shift) % n_rows, 0, False))
        d = n_rows - shift
        hop = (d % (n_rows - 1) + 1 - d) % n_rows
        own_blk = lax.dynamic_slice_in_dim(block, level * rows, rows, axis=-1)
        next_blk = lax.dynamic_slice_in_dim(
            block, ((level + hop) % n_rows) * rows, rows, axis=-1
        )
        pairs = [(a, (a + shift) % n_rows) for a in range(n_rows)]
        ladder_in.append(
            lax.ppermute(jnp.concatenate([own_blk, next_blk], axis=-1), "row", pairs)
        )
    dest = jnp.arange(n_chan, dtype=jnp.int32)
    q_dest = level * n_chan + dest
    slot_dest = src_slot[q_dest, mine]
    part_dest = q_dest // ch_dev - level * (rows // slab)
    outgoing = pair(lambda x: x.reshape(ch_dev, rows // slab, slab, width)[slot_dest, part_dest])
    arrived = lax.all_to_all(outgoing, "ch", split_axis=1, concat_axis=1, tiled=True)
    a_eta = arrived[0].reshape(width, width)
    b_gamma = arrived[1].reshape(width, width)

    perm = [(q, (q % n_chan) * n_rows + q // n_chan) for q in range(n_total)]
    coefs = lax.ppermute(
        jnp.concatenate([ph_factor.astype(f32), recouple], axis=0), ("ch", "row"), perm
    )
    weight = coefs[0].astype(bf16)[None, :]
    coef = coefs[1]

    a_w = a_eta * weight
    b_w = b_gamma * weight
    parts = []
    for r in range(n_rows):
        cut = slice(r * rows, (r + 1) * rows)
        part = jnp.dot(a_w, b_gamma[:, cut], preferred_element_type=f32)
        part = part - jnp.dot(b_w, a_eta[:, cut], preferred_element_type=f32)
        parts.append((part * coef[:, None]).astype(bf16).reshape(n_chan, slab, rows))
    term_t = jnp.stack(parts, axis=1)
    ladder_in, _ = lax.optimization_barrier((ladder_in, term_t))
    sign = jnp.array([-1, 1], bf16)[:, None, None]
    own = pair(lambda x: lax.dynamic_index_in_dim(x, level, 0, False))
    own = jnp.roll(own, -level * rows, axis=-1)
    grid = [[None] * n_rows for _ in range(n_rows)]
    for d in range(n_rows):
        grid[0][d] = own[..., d * rows : (d + 1) * rows]
    for d in range(1, n_rows):
        piece = ladder_in[n_rows - d - 1]
        succ = d % (n_rows - 1) + 1
        grid[d][0] = sign * jnp.swapaxes(grid[0][d], -1, -2)
        grid[d][d] = piece[..., :rows]
        grid[d][succ] = piece[..., rows:]
        grid[succ][d] = sign * jnp.swapaxes(piece[..., rows:], -1, -2)
    whole = jnp.concatenate([jnp.concatenate(line, axis=-1) for line in grid], axis=-2)
    factor = lax.dynamic_index_in_dim(pp_factor, level, 0, False).astype(bf16)
    factor = jnp.roll(factor, -level * rows)
    left = jnp.concatenate([whole[0] * factor, whole[1] * factor], axis=-1)
    right = jnp.concatenate([whole[1], whole[0]], axis=-1)
    ladder_c = lax.dot_general(
        left, right, (((1,), (1,)), ((), ())), preferred_element_type=f32
    ).reshape(n_rows, rows, width)
    sending = jnp.stack([skip_block(ladder_c[a], a, rows) for a in range(n_rows)])
    returning = term_t
    landed = lax.all_to_all(
        returning.reshape(n_chan * n_rows, slab, rows),
        ("ch", "row"),
        split_axis=0,
        concat_axis=0,
        tiled=True,
    )
    landed = landed.reshape(n_chan, n_rows, slab, rows).transpose(1, 0, 2, 3)
    landed = landed.reshape(n_chan, ch_dev, slab, rows)
    returned = [sending[0]]
    for shift in range(1, n_rows):
        pairs = [(a, (a + shift) % n_rows) for a in range(n_rows)]
        returned.append(lax.ppermute(sending[shift], "row", pairs))
    ladder = jnp.stack(
        [lax.select_n((level - s) % n_rows, *returned) for s in range(n_rows)]
    )
    chosen = src_slot[:, mine].reshape(n_chan, ch_dev)
    onehot = (chosen[:, :, None] == jnp.arange(ch_dev, dtype=jnp.int32)[None, None, :]).astype(bf16)
    back = jnp.einsum("gts,gtwi->sigw", onehot, landed, preferred_element_type=f32)
    back = back.reshape(ch_dev, rows, width)

    local_d = pp_factor.astype(bf16)[:, None, :]
    left = jnp.concatenate([eta_pp * local_d, gamma_pp * local_d], axis=-1)
    right = jnp.concatenate([gamma_pp, eta_pp], axis=-1)
    diag = jnp.einsum("sik,sjk->sij", left, right, preferred_element_type=f32)
    ladder = jnp.concatenate([ladder, diag], axis=-1)
    ladder = jnp.roll(ladder, (level + 1) * rows, axis=-1)
    return (ladder + back).astype(bf16)


def solution(mesh):
    placed = (
        P("ch", "row", None),
        P("ch", "row", None),
        P("ch", None),
        P(("ch", "row"), None),
        P(("ch", "row"), None),
        P(),
    )
    return jax.shard_map(
        per_device, mesh=mesh, in_specs=placed, out_specs=P("ch", "row", None), check_vma=False
    )
```

```python
import jax
import jax.numpy as jnp
from jax import lax
from jax.sharding import PartitionSpec as P


def skip_block(x, b, size):
    return jnp.concatenate([x[..., (b + 1) * size :], x[..., : b * size]], axis=-1)


def per_device(eta_pp, gamma_pp, pp_factor, ph_factor, recouple, src_slot):
    f32 = jnp.float32
    bf16 = jnp.bfloat16
    n_chan = lax.axis_size("ch")
    n_rows = lax.axis_size("row")
    ch_dev, rows, width = eta_pp.shape
    slab = width // n_chan
    n_total = ch_dev * n_chan
    assert ch_dev == n_rows and rows % slab == 0 and n_chan * slab == width
    mine = lax.axis_index("ch")
    level = lax.axis_index("row")

    assert n_rows == 4
    pair = lambda f: jnp.stack([f(eta_pp), f(gamma_pp)])
    ladder_in = []
    for shift in range(1, n_rows):
        block = pair(lambda x: lax.dynamic_index_in_dim(x, (level + shift) % n_rows, 0, False))
        d = n_rows - shift
        hop = (d % (n_rows - 1) + 1 - d) % n_rows
        own_blk = lax.dynamic_slice_in_dim(block, level * rows, rows, axis=-1)
        next_blk = lax.dynamic_slice_in_dim(
            block, ((level + hop) % n_rows) * rows, rows, axis=-1
        )
        pairs = [(a, (a + shift) % n_rows) for a in range(n_rows)]
        ladder_in.append(
            lax.ppermute(jnp.concatenate([own_blk, next_blk], axis=-1), "row", pairs)
        )
    dest = jnp.arange(n_chan, dtype=jnp.int32)
    q_dest = level * n_chan + dest
    slot_dest = src_slot[q_dest, mine]
    part_dest = q_dest // ch_dev - level * (rows // slab)
    outgoing = pair(lambda x: x.reshape(ch_dev, rows // slab, slab, width)[slot_dest, part_dest])
    arrived = lax.all_to_all(outgoing, "ch", split_axis=1, concat_axis=1, tiled=True)
    a_eta = arrived[0].reshape(width, width)
    b_gamma = arrived[1].reshape(width, width)

    perm = [(q, (q % n_chan) * n_rows + q // n_chan) for q in range(n_total)]
    coefs = lax.ppermute(
        jnp.concatenate([ph_factor.astype(f32), recouple], axis=0), ("ch", "row"), perm
    )
    weight = coefs[0].astype(bf16)[None, :]
    coef = coefs[1]

    a_w = a_eta * weight
    b_w = b_gamma * weight
    parts = []
    for r in range(n_rows):
        cut = slice(r * rows, (r + 1) * rows)
        part = jnp.dot(a_w, b_gamma[:, cut], preferred_element_type=f32)
        part = part - jnp.dot(b_w, a_eta[:, cut], preferred_element_type=f32)
        parts.append((part * coef[:, None]).astype(bf16).reshape(n_chan, slab, rows))
    term_t = jnp.stack(parts, axis=1)
    sign = jnp.array([-1, 1], bf16)[:, None, None]
    own = pair(lambda x: lax.dynamic_index_in_dim(x, level, 0, False))
    own = jnp.roll(own, -level * rows, axis=-1)
    grid = [[None] * n_rows for _ in range(n_rows)]
    for d in range(n_rows):
        grid[0][d] = own[..., d * rows : (d + 1) * rows]
    for d in range(1, n_rows):
        piece = ladder_in[n_rows - d - 1]
        succ = d % (n_rows - 1) + 1
        grid[d][0] = sign * jnp.swapaxes(grid[0][d], -1, -2)
        grid[d][d] = piece[..., :rows]
        grid[d][succ] = piece[..., rows:]
        grid[succ][d] = sign * jnp.swapaxes(piece[..., rows:], -1, -2)
    whole = jnp.concatenate([jnp.concatenate(line, axis=-1) for line in grid], axis=-2)
    factor = lax.dynamic_index_in_dim(pp_factor, level, 0, False).astype(bf16)
    factor = jnp.roll(factor, -level * rows)
    left = jnp.concatenate([whole[0] * factor, whole[1] * factor], axis=-1)
    right = jnp.concatenate([whole[1], whole[0]], axis=-1)
    ladder_c = lax.dot_general(
        left, right, (((1,), (1,)), ((), ())), preferred_element_type=f32
    ).reshape(n_rows, rows, width)
    sending = jnp.stack([skip_block(ladder_c[a], a, rows) for a in range(n_rows)])
    returning = term_t
    landed = lax.all_to_all(
        returning.reshape(n_chan * n_rows, slab, rows),
        ("ch", "row"),
        split_axis=0,
        concat_axis=0,
        tiled=True,
    )
    landed = landed.reshape(n_chan, n_rows, slab, rows).transpose(1, 0, 2, 3)
    landed = landed.reshape(n_chan, ch_dev, slab, rows)
    returned = [sending[0]]
    for shift in range(1, n_rows):
        pairs = [(a, (a + shift) % n_rows) for a in range(n_rows)]
        returned.append(lax.ppermute(sending[shift], "row", pairs))
    ladder = jnp.stack(
        [lax.select_n((level - s) % n_rows, *returned) for s in range(n_rows)]
    )
    chosen = src_slot[:, mine].reshape(n_chan, ch_dev)
    onehot = (chosen[:, :, None] == jnp.arange(ch_dev, dtype=jnp.int32)[None, None, :]).astype(bf16)
    back = jnp.einsum("gts,gtwi->sigw", onehot, landed, preferred_element_type=f32)
    back = back.reshape(ch_dev, rows, width)

    local_d = pp_factor.astype(bf16)[:, None, :]
    left = jnp.concatenate([eta_pp * local_d, gamma_pp * local_d], axis=-1)
    right = jnp.concatenate([gamma_pp, eta_pp], axis=-1)
    diag = jnp.einsum("sik,sjk->sij", left, right, preferred_element_type=f32)
    ladder = jnp.concatenate([ladder, diag], axis=-1)
    ladder = jnp.roll(ladder, (level + 1) * rows, axis=-1)
    return (ladder + back).astype(bf16)


def solution(mesh):
    placed = (
        P("ch", "row", None),
        P("ch", "row", None),
        P("ch", None),
        P(("ch", "row"), None),
        P(("ch", "row"), None),
        P(),
    )
    return jax.shard_map(
        per_device, mesh=mesh, in_specs=placed, out_specs=P("ch", "row", None), check_vma=False
    )
```

```python
import jax
import jax.numpy as jnp
from jax import lax
from jax.sharding import PartitionSpec as P


def skip_block(x, b, size):
    return jnp.concatenate([x[..., (b + 1) * size :], x[..., : b * size]], axis=-1)


def per_device(eta_pp, gamma_pp, pp_factor, ph_factor, recouple, src_slot):
    f32 = jnp.float32
    bf16 = jnp.bfloat16
    n_chan = lax.axis_size("ch")
    n_rows = lax.axis_size("row")
    ch_dev, rows, width = eta_pp.shape
    slab = width // n_chan
    n_total = ch_dev * n_chan
    assert ch_dev == n_rows and rows % slab == 0 and n_chan * slab == width
    mine = lax.axis_index("ch")
    level = lax.axis_index("row")

    assert n_rows == 4
    pair = lambda f: jnp.stack([f(eta_pp), f(gamma_pp)])
    ladder_in = []
    for shift in range(1, n_rows):
        block = pair(lambda x: lax.dynamic_index_in_dim(x, (level + shift) % n_rows, 0, False))
        d = n_rows - shift
        hop = (d % (n_rows - 1) + 1 - d) % n_rows
        own_blk = lax.dynamic_slice_in_dim(block, level * rows, rows, axis=-1)
        next_blk = lax.dynamic_slice_in_dim(
            block, ((level + hop) % n_rows) * rows, rows, axis=-1
        )
        pairs = [(a, (a + shift) % n_rows) for a in range(n_rows)]
        ladder_in.append(
            lax.ppermute(jnp.concatenate([own_blk, next_blk], axis=-1), "row", pairs)
        )
    dest = jnp.arange(n_chan, dtype=jnp.int32)
    q_dest = level * n_chan + dest
    slot_dest = src_slot[q_dest, mine]
    part_dest = q_dest // ch_dev - level * (rows // slab)
    outgoing = pair(lambda x: x.reshape(ch_dev, rows // slab, slab, width)[slot_dest, part_dest])
    arrived = lax.all_to_all(outgoing, "ch", split_axis=1, concat_axis=1, tiled=True)
    a_eta = arrived[0].reshape(width, width)
    b_gamma = arrived[1].reshape(width, width)

    perm = [(q, (q % n_chan) * n_rows + q // n_chan) for q in range(n_total)]
    coefs = lax.ppermute(
        jnp.concatenate([ph_factor.astype(f32), recouple], axis=0), ("ch", "row"), perm
    )
    weight = coefs[0].astype(bf16)[None, :]
    coef = coefs[1]

    lhs = jnp.concatenate([a_eta * weight, b_gamma * weight], axis=1)
    rhs = jnp.concatenate([b_gamma, -a_eta], axis=0)
    parts = []
    for r in range(n_rows):
        part = jnp.dot(lhs, rhs[:, r * rows : (r + 1) * rows], preferred_element_type=f32)
        parts.append((part * coef[:, None]).astype(bf16).reshape(n_chan, slab, rows))
    term_t = jnp.stack(parts, axis=1)
    ladder_in, _ = lax.optimization_barrier((ladder_in, term_t))
    sign = jnp.array([-1, 1], bf16)[:, None, None]
    own = pair(lambda x: lax.dynamic_index_in_dim(x, level, 0, False))
    own = jnp.roll(own, -level * rows, axis=-1)
    grid = [[None] * n_rows for _ in range(n_rows)]
    for d in range(n_rows):
        grid[0][d] = own[..., d * rows : (d + 1) * rows]
    for d in range(1, n_rows):
        piece = ladder_in[n_rows - d - 1]
        succ = d % (n_rows - 1) + 1
        grid[d][0] = sign * jnp.swapaxes(grid[0][d], -1, -2)
        grid[d][d] = piece[..., :rows]
        grid[d][succ] = piece[..., rows:]
        grid[succ][d] = sign * jnp.swapaxes(piece[..., rows:], -1, -2)
    whole = jnp.concatenate([jnp.concatenate(line, axis=-1) for line in grid], axis=-2)
    factor = lax.dynamic_index_in_dim(pp_factor, level, 0, False).astype(bf16)
    factor = jnp.roll(factor, -level * rows)
    left = jnp.concatenate([whole[0] * factor, whole[1] * factor], axis=-1)
    right = jnp.concatenate([whole[1], whole[0]], axis=-1)
    ladder_c = lax.dot_general(
        left, right, (((1,), (1,)), ((), ())), preferred_element_type=f32
    ).reshape(n_rows, rows, width)
    sending = jnp.stack([skip_block(ladder_c[a], a, rows) for a in range(n_rows)])
    returning = term_t
    landed = lax.all_to_all(
        returning.reshape(n_chan * n_rows, slab, rows),
        ("ch", "row"),
        split_axis=0,
        concat_axis=0,
        tiled=True,
    )
    landed = landed.reshape(n_chan, n_rows, slab, rows).transpose(1, 0, 2, 3)
    landed = landed.reshape(n_chan, ch_dev, slab, rows)
    returned = [sending[0]]
    for shift in range(1, n_rows):
        pairs = [(a, (a + shift) % n_rows) for a in range(n_rows)]
        returned.append(lax.ppermute(sending[shift], "row", pairs))
    ladder = jnp.stack(
        [lax.select_n((level - s) % n_rows, *returned) for s in range(n_rows)]
    )
    chosen = src_slot[:, mine].reshape(n_chan, ch_dev)
    onehot = (chosen[:, :, None] == jnp.arange(ch_dev, dtype=jnp.int32)[None, None, :]).astype(bf16)
    back = jnp.einsum("gts,gtwi->sigw", onehot, landed, preferred_element_type=f32)
    back = back.reshape(ch_dev, rows, width)

    local_d = pp_factor.astype(bf16)[:, None, :]
    left = jnp.concatenate([eta_pp * local_d, gamma_pp * local_d], axis=-1)
    right = jnp.concatenate([gamma_pp, eta_pp], axis=-1)
    diag = jnp.einsum("sik,sjk->sij", left, right, preferred_element_type=f32)
    ladder = jnp.concatenate([ladder, diag], axis=-1)
    ladder = jnp.roll(ladder, (level + 1) * rows, axis=-1)
    return (ladder + back).astype(bf16)


def solution(mesh):
    placed = (
        P("ch", "row", None),
        P("ch", "row", None),
        P("ch", None),
        P(("ch", "row"), None),
        P(("ch", "row"), None),
        P(),
    )
    return jax.shard_map(
        per_device, mesh=mesh, in_specs=placed, out_specs=P("ch", "row", None), check_vma=False
    )
```

```python
import jax
import jax.numpy as jnp
from jax import lax
from jax.sharding import PartitionSpec as P


def skip_block(x, b, size):
    return jnp.concatenate([x[..., (b + 1) * size :], x[..., : b * size]], axis=-1)


def per_device(eta_pp, gamma_pp, pp_factor, ph_factor, recouple, src_slot):
    f32 = jnp.float32
    bf16 = jnp.bfloat16
    n_chan = lax.axis_size("ch")
    n_rows = lax.axis_size("row")
    ch_dev, rows, width = eta_pp.shape
    slab = width // n_chan
    n_total = ch_dev * n_chan
    assert ch_dev == n_rows and rows % slab == 0 and n_chan * slab == width
    mine = lax.axis_index("ch")
    level = lax.axis_index("row")

    assert n_rows == 4
    pair = lambda f: jnp.stack([f(eta_pp), f(gamma_pp)])
    ladder_in = []
    for shift in range(1, n_rows):
        block = pair(lambda x: lax.dynamic_index_in_dim(x, (level + shift) % n_rows, 0, False))
        d = n_rows - shift
        hop = (d % (n_rows - 1) + 1 - d) % n_rows
        own_blk = lax.dynamic_slice_in_dim(block, level * rows, rows, axis=-1)
        next_blk = lax.dynamic_slice_in_dim(
            block, ((level + hop) % n_rows) * rows, rows, axis=-1
        )
        pairs = [(a, (a + shift) % n_rows) for a in range(n_rows)]
        ladder_in.append(
            lax.ppermute(jnp.concatenate([own_blk, next_blk], axis=-1), "row", pairs)
        )
    dest = jnp.arange(n_chan, dtype=jnp.int32)
    q_dest = level * n_chan + dest
    slot_dest = src_slot[q_dest, mine]
    part_dest = q_dest // ch_dev - level * (rows // slab)
    slabs = lambda x: lax.all_to_all(
        x.reshape(ch_dev, rows // slab, slab, width)[slot_dest, part_dest],
        "ch", split_axis=0, concat_axis=0, tiled=True,
    )
    a_eta = slabs(eta_pp).reshape(width, width)
    b_gamma = slabs(gamma_pp).reshape(width, width)

    perm = [(q, (q % n_chan) * n_rows + q // n_chan) for q in range(n_total)]
    coefs = lax.ppermute(
        jnp.concatenate([ph_factor.astype(f32), recouple], axis=0), ("ch", "row"), perm
    )
    weight = coefs[0].astype(bf16)[None, :]
    coef = coefs[1]

    a_w = a_eta * weight
    b_w = b_gamma * weight
    parts = []
    for r in range(n_rows):
        cut = slice(r * rows, (r + 1) * rows)
        part = jnp.dot(a_w, b_gamma[:, cut], preferred_element_type=f32)
        part = part - jnp.dot(b_w, a_eta[:, cut], preferred_element_type=f32)
        parts.append((part * coef[:, None]).astype(bf16).reshape(n_chan, slab, rows))
    term_t = jnp.stack(parts, axis=1)
    ladder_in, _ = lax.optimization_barrier((ladder_in, term_t))
    sign = jnp.array([-1, 1], bf16)[:, None, None]
    own = pair(lambda x: lax.dynamic_index_in_dim(x, level, 0, False))
    own = jnp.roll(own, -level * rows, axis=-1)
    grid = [[None] * n_rows for _ in range(n_rows)]
    for d in range(n_rows):
        grid[0][d] = own[..., d * rows : (d + 1) * rows]
    for d in range(1, n_rows):
        piece = ladder_in[n_rows - d - 1]
        succ = d % (n_rows - 1) + 1
        grid[d][0] = sign * jnp.swapaxes(grid[0][d], -1, -2)
        grid[d][d] = piece[..., :rows]
        grid[d][succ] = piece[..., rows:]
        grid[succ][d] = sign * jnp.swapaxes(piece[..., rows:], -1, -2)
    whole = jnp.concatenate([jnp.concatenate(line, axis=-1) for line in grid], axis=-2)
    factor = lax.dynamic_index_in_dim(pp_factor, level, 0, False).astype(bf16)
    factor = jnp.roll(factor, -level * rows)
    left = jnp.concatenate([whole[0] * factor, whole[1] * factor], axis=-1)
    right = jnp.concatenate([whole[1], whole[0]], axis=-1)
    ladder_c = lax.dot_general(
        left, right, (((1,), (1,)), ((), ())), preferred_element_type=f32
    ).reshape(n_rows, rows, width)
    sending = jnp.stack([skip_block(ladder_c[a], a, rows) for a in range(n_rows)])
    returning = term_t
    landed = lax.all_to_all(
        returning.reshape(n_chan * n_rows, slab, rows),
        ("ch", "row"),
        split_axis=0,
        concat_axis=0,
        tiled=True,
    )
    landed = landed.reshape(n_chan, n_rows, slab, rows).transpose(1, 0, 2, 3)
    landed = landed.reshape(n_chan, ch_dev, slab, rows)
    returned = [sending[0]]
    for shift in range(1, n_rows):
        pairs = [(a, (a + shift) % n_rows) for a in range(n_rows)]
        returned.append(lax.ppermute(sending[shift], "row", pairs))
    ladder = jnp.stack(
        [lax.select_n((level - s) % n_rows, *returned) for s in range(n_rows)]
    )
    chosen = src_slot[:, mine].reshape(n_chan, ch_dev)
    onehot = (chosen[:, :, None] == jnp.arange(ch_dev, dtype=jnp.int32)[None, None, :]).astype(bf16)
    back = jnp.einsum("gts,gtwi->sigw", onehot, landed, preferred_element_type=f32)
    back = back.reshape(ch_dev, rows, width)

    local_d = pp_factor.astype(bf16)[:, None, :]
    left = jnp.concatenate([eta_pp * local_d, gamma_pp * local_d], axis=-1)
    right = jnp.concatenate([gamma_pp, eta_pp], axis=-1)
    diag = jnp.einsum("sik,sjk->sij", left, right, preferred_element_type=f32)
    ladder = jnp.concatenate([ladder, diag], axis=-1)
    ladder = jnp.roll(ladder, (level + 1) * rows, axis=-1)
    return (ladder + back).astype(bf16)


def solution(mesh):
    placed = (
        P("ch", "row", None),
        P("ch", "row", None),
        P("ch", None),
        P(("ch", "row"), None),
        P(("ch", "row"), None),
        P(),
    )
    return jax.shard_map(
        per_device, mesh=mesh, in_specs=placed, out_specs=P("ch", "row", None), check_vma=False
    )
```
